256 devices in a mesh: seg: 64 (over z, y, x_hi), frm: 2 (over core), rec: 2 (over x_lo).
Axes of the slice: x: 4 (x_hi: 2, x_lo: 2; x = x_hi * 2 + x_lo), y: 4, z: 8, core: 2. Of those that a mesh axis runs over, the one named last changes fastest.
Arguments:
- frames_in: bfloat16 [2, 32768, 1024], P('rec', ('seg', 'frm')), may hold values from -12 to 12
- w_qkv: bfloat16 [1024, 3072], replicated, may hold values from -0.1875 to 0.1875
- w_out: bfloat16 [1024, 1024], replicated, may hold values from -0.1875 to 0.1875
Outputs:
- attended: bfloat16 [2, 32768, 1024], P('rec', ('seg', 'frm'))
The draws below stay inside these ranges and needn't reach their ends.
All inputs are finite; a program needn't handle non-finite values.
Results may differ from the reference program's by a relative error of at most 0.0051.
Values may be sent and summed in bfloat16 or wider, within the bound.
No kernel may reach another device: no remote copies, remote signals or barrier semaphores. Data moves between devices by JAX's collectives and lax.ppermute only.
A program may use at most 192 MiB of HBM per device.

```python
import jax
import jax.numpy as jnp
from jax import lax

D = 1024
HEADS = 16
HEAD_DIM = 64
SPAN = 256
TOK_DEV = 256
FRAMES = 32768
RECS = 2


def draw_frames_in(key, part):
    key_noise = jax.random.fold_in(key, 11)
    key_offset = jax.random.fold_in(key, 12)
    blocks = FRAMES // TOK_DEV
    offset = jax.random.normal(key_offset, (RECS, blocks, 1, D), jnp.float32) * 1.5
    offset = jnp.broadcast_to(offset, (RECS, blocks, TOK_DEV, D)).reshape(RECS, FRAMES, D)
    noise = jax.random.normal(key_noise, (RECS, FRAMES, D), jnp.float32)
    return jnp.clip(noise + offset, -12.0, 12.0).astype(jnp.bfloat16)


def gaussian(key, dims, deviation, most, dtype=jnp.bfloat16):
    values = deviation * jax.random.normal(key, dims, jnp.float32)
    return jnp.clip(values, min=-most, max=most).astype(dtype)


def setup_inputs(seed: int = 0) -> dict:
    streams_of = jax.random.split(jax.random.key(seed), 4)
    frames_in = draw_frames_in(jax.random.fold_in(streams_of[3], 71), 0)
    w_qkv = gaussian(streams_of[1], (D, 3 * D), D ** -0.5, 0.1875)
    w_out = gaussian(streams_of[2], (D, D), D ** -0.5, 0.1875)
    return {"frames_in": frames_in, "w_qkv": w_qkv, "w_out": w_out}


def features(t):
    return jnp.where(t > 0.0, t + 1.0, jnp.exp(jnp.minimum(t, 0.0)))


def block_output(phi_q, phi_k, values, prior_kv, prior_k, span):
    rows, length, heads, dim = phi_q.shape
    count = length // span
    pq = phi_q.reshape(rows, count, span, heads, dim)
    pk = phi_k.reshape(rows, count, span, heads, dim)
    vv = values.reshape(rows, count, span, heads, dim)
    scores = jnp.einsum("rnihd,rnjhd->rnhij", pq.astype(jnp.float32), pk.astype(jnp.float32))
    causal = jnp.arange(span)[:, None] >= jnp.arange(span)[None, :]
    scores = jnp.where(causal, scores, 0.0)
    den_local = jnp.sum(scores, axis=-1)
    weights = scores.astype(jnp.bfloat16)
    num_local = jnp.einsum("rnhij,rnjhd->rnihd", weights.astype(jnp.float32), vv.astype(jnp.float32))
    kv_blocks = jnp.einsum("rnjhd,rnjhe->rnhde", pk.astype(jnp.float32), vv.astype(jnp.float32))
    k_blocks = jnp.sum(pk.astype(jnp.float32), axis=2)
    before_kv = jnp.cumsum(kv_blocks, axis=1) - kv_blocks + prior_kv[:, None]
    before_k = jnp.cumsum(k_blocks, axis=1) - k_blocks + prior_k[:, None]
    pq32 = pq.astype(jnp.float32)
    num = num_local + jnp.einsum("rnihd,rnhde->rnihe", pq32, before_kv, precision=lax.Precision.HIGHEST)
    den = jnp.transpose(den_local, (0, 1, 3, 2)) + jnp.einsum("rnihd,rnhd->rnih", pq32, before_k, precision=lax.Precision.HIGHEST)
    result = (num / den[..., None]).astype(jnp.bfloat16)
    return result.reshape(rows, length, heads * dim)


def one_recording(frames, w_qkv, w_out):
    qkv = jnp.dot(frames, w_qkv, preferred_element_type=jnp.float32).astype(jnp.bfloat16)
    qkv = qkv.reshape(1, FRAMES, 3, HEADS, HEAD_DIM)
    phi_q = features(qkv[:, :, 0].astype(jnp.float32)).astype(jnp.bfloat16)
    phi_k = features(qkv[:, :, 1].astype(jnp.float32)).astype(jnp.bfloat16)
    values = qkv[:, :, 2]
    prior_kv = jnp.zeros((1, HEADS, HEAD_DIM, HEAD_DIM), jnp.float32)
    prior_k = jnp.zeros((1, HEADS, HEAD_DIM), jnp.float32)
    heads_out = block_output(phi_q, phi_k, values, prior_kv, prior_k, SPAN)[0]
    return jnp.dot(heads_out, w_out, preferred_element_type=jnp.float32).astype(jnp.bfloat16)


def reference(frames_in, w_qkv, w_out):
    return lax.map(lambda frames: one_recording(frames, w_qkv, w_out), frames_in)
```

```python
import jax
import jax.numpy as jnp
from jax import lax
from jax.sharding import Mesh, PartitionSpec as P

HEADS = 16
SPAN = 256

SEG_SPLIT = (("seg_z", 8), ("seg_y", 4), ("seg_x", 2))
SCAN_AXES = ("seg_z", "seg_y", "seg_x", "frm")


def features(t):
    return jnp.where(t > 0.0, t + 1.0, jnp.exp(jnp.minimum(t, 0.0)))


def tmap(f, *trees):
    return jax.tree.map(f, *trees)


def swap(tree, axis):
    return tmap(lambda t: lax.ppermute(t, axis, perm=[(0, 1), (1, 0)]), tree)


def part(tree, index, count):
    def one(t):
        size = t.shape[0] // count
        return lax.dynamic_slice_in_dim(t, index * size, size, axis=0)

    return tmap(one, tree)


def gather(tree, axis, tiled):
    return tmap(lambda t: lax.all_gather(t, axis, axis=0, tiled=tiled), tree)


def before_and_total(stack, mine):
    def one(s):
        n = s.shape[0]
        idx = lax.broadcasted_iota(jnp.int32, s.shape, 0)
        before = jnp.sum(jnp.where(idx < mine, s, 0.0), axis=0)
        return before, jnp.sum(s, axis=0)

    pairs = tmap(one, stack)
    is_pair = lambda x: isinstance(x, tuple) and len(x) == 2 and not isinstance(x[0], tuple)
    before = jax.tree.map(lambda p: p[0], pairs, is_leaf=is_pair)
    total = jax.tree.map(lambda p: p[1], pairs, is_leaf=is_pair)
    return before, total


def ordered(mine, other, first):
    lo = tmap(lambda a, b: jnp.where(first, a, b), mine, other)
    hi = tmap(lambda a, b: jnp.where(first, b, a), mine, other)
    return lo, hi


def entering(total):
    core = lax.axis_index("frm")
    xh = lax.axis_index("seg_x")
    y = lax.axis_index("seg_y")
    z = lax.axis_index("seg_z")
    lo, hi = ordered(total, swap(total, "frm"), core == 0)
    own_core = tmap(lambda a: jnp.where(core == 1, a, 0.0), lo)
    chip = part(tmap(jnp.add, lo, hi), core, 2)
    lo, hi = ordered(chip, swap(chip, "seg_x"), xh == 0)
    own_x = tmap(lambda a: jnp.where(xh == 1, a, 0.0), lo)
    row = part(tmap(jnp.add, lo, hi), xh, 2)
    own_y, plane = before_and_total(gather(row, "seg_y", False), y)
    own_z, _ = before_and_total(gather(part(plane, y, 4), "seg_z", False), z)
    quarter = tmap(jnp.add, gather(own_z, "seg_y", True), own_y)
    half = tmap(jnp.add, gather(quarter, "seg_x", True), own_x)
    return tmap(jnp.add, gather(half, "frm", True), own_core)


def block_terms(phi_q, phi_k, values, span):
    rows, length, heads, dim = phi_q.shape
    count = length // span
    pq = phi_q.reshape(rows, count, span, heads, dim)
    pk = phi_k.reshape(rows, count, span, heads, dim)
    vv = values.reshape(rows, count, span, heads, dim)
    scores = jnp.einsum("rnihd,rnjhd->rnhij", pq, pk, preferred_element_type=jnp.float32)
    causal = jnp.arange(span)[:, None] >= jnp.arange(span)[None, :]
    scores = jnp.where(causal, scores, 0.0)
    den_local = jnp.sum(scores, axis=-1)
    weights = scores.astype(jnp.bfloat16)
    num_local = jnp.einsum("rnhij,rnjhd->rnihd", weights, vv, preferred_element_type=jnp.float32)
    kv_blocks = jnp.einsum("rnjhd,rnjhe->rnhde", pk, vv, preferred_element_type=jnp.float32)
    k_blocks = jnp.sum(pk, axis=2, dtype=jnp.float32)
    return (pq, num_local, den_local, kv_blocks, k_blocks)


def finish(pq, num_local, den_local, kv_blocks, k_blocks, prior_kv, prior_k):
    rows, count, span, heads, dim = pq.shape
    before_kv = jnp.cumsum(kv_blocks, axis=1) - kv_blocks + prior_kv[:, None]
    before_k = jnp.cumsum(k_blocks, axis=1) - k_blocks + prior_k[:, None]
    pq32 = pq.astype(jnp.float32)
    num = num_local + jnp.einsum(
        "rnihd,rnhde->rnihe", pq32, before_kv, precision=lax.Precision.HIGHEST
    )
    den = jnp.transpose(den_local, (0, 1, 3, 2)) + jnp.einsum(
        "rnihd,rnhd->rnih", pq32, before_k, precision=lax.Precision.HIGHEST
    )
    result = (num / den[..., None]).astype(jnp.bfloat16)
    return result.reshape(rows, count * span, heads * dim)


def split_qkv(qkv):
    phi_q = features(qkv[:, :, 0].astype(jnp.float32)).astype(jnp.bfloat16)
    phi_k = features(qkv[:, :, 1].astype(jnp.float32)).astype(jnp.bfloat16)
    return (phi_q, phi_k, qkv[:, :, 2])


def shards(frames_in, w_qkv, w_out):
    rows, tok_local, width = frames_in.shape
    head_dim = width // HEADS
    qkv = jnp.einsum("rtd,de->rte", frames_in, w_qkv, preferred_element_type=jnp.float32).astype(
        jnp.bfloat16
    )
    parts = qkv.reshape(rows, tok_local, 3, HEADS, head_dim)
    phi_q, phi_k, values = split_qkv(parts)
    pq, num_local, den_local, kv_blocks, k_blocks = block_terms(phi_q, phi_k, values, SPAN)
    total_kv = jnp.sum(kv_blocks, axis=1)[0]
    total_k = jnp.sum(k_blocks, axis=1)[0]
    prior_kv, prior_k = entering((total_kv, total_k))
    heads_out = finish(
        pq, num_local, den_local, kv_blocks, k_blocks, prior_kv[None], prior_k[None]
    )
    return jnp.einsum("rtd,de->rte", heads_out, w_out, preferred_element_type=jnp.float32).astype(
        jnp.bfloat16
    )


def solution(mesh):
    sizes = [n for _, n in SEG_SPLIT]
    devices = mesh.devices.reshape(
        *sizes, mesh.shape["frm"], mesh.shape["rec"]
    )
    fine = Mesh(devices, tuple(name for name, _ in SEG_SPLIT) + ("frm", "rec"))
    in_specs = (P("rec", SCAN_AXES, None), P(), P())
    out_specs = P("rec", SCAN_AXES, None)
    return jax.shard_map(shards, mesh=fine, in_specs=in_specs, out_specs=out_specs, check_vma=False)
```

```python
import jax
import jax.numpy as jnp
from jax import lax
from jax.sharding import Mesh, PartitionSpec as P

HEADS = 16
SPAN = 256

SEG_SPLIT = (("seg_z", 8), ("seg_y", 4), ("seg_x", 2))
SCAN_AXES = ("seg_z", "seg_y", "seg_x", "frm")


def features(t):
    return jnp.where(t > 0.0, t + 1.0, jnp.exp(jnp.minimum(t, 0.0)))


def tmap(f, *trees):
    return jax.tree.map(f, *trees)


def send(tree, axis, pairs):
    return tmap(lambda t: lax.ppermute(t, axis, perm=pairs), tree)


def swap(tree, axis):
    return send(tree, axis, [(0, 1), (1, 0)])


def forward(n, s):
    return [(i, i + s) for i in range(n - s)]


def part(tree, index, count):
    def one(t):
        size = t.shape[0] // count
        return lax.dynamic_slice_in_dim(t, index * size, size, axis=0)

    return tmap(one, tree)


def ordered(mine, other, first):
    lo = tmap(lambda a, b: jnp.where(first, a, b), mine, other)
    hi = tmap(lambda a, b: jnp.where(first, b, a), mine, other)
    return lo, hi


def keep(tree, cond):
    return tmap(lambda a: jnp.where(cond, a, jnp.zeros_like(a)), tree)


def joined(lo, hi):
    return tmap(lambda a, b: jnp.concatenate([a, b], axis=0), lo, hi)


def entering(total):
    core = lax.axis_index("frm")
    xh = lax.axis_index("seg_x")
    y = lax.axis_index("seg_y")
    z = lax.axis_index("seg_z")
    n_y = lax.axis_size("seg_y")
    n_z = lax.axis_size("seg_z")
    lo, hi = ordered(total, swap(total, "frm"), core == 0)
    own_core = keep(lo, core == 1)
    chip = part(tmap(jnp.add, lo, hi), core, 2)
    lo, hi = ordered(chip, swap(chip, "seg_x"), xh == 0)
    own_x = keep(lo, xh == 1)
    row = part(tmap(jnp.add, lo, hi), xh, 2)
    own_y = tmap(jnp.zeros_like, row)
    plane = part(row, y, n_y)
    for s in range(1, n_y):
        early = send(row, "seg_y", forward(n_y, s))
        own_y = tmap(jnp.add, own_y, early)
        plane = tmap(jnp.add, plane, part(early, y, n_y))
        late = send(part(row, jnp.maximum(y - s, 0), n_y), "seg_y", [(i + s, i) for i in range(n_y - s)])
        plane = tmap(jnp.add, plane, late)
    own_z = tmap(jnp.zeros_like, plane)
    for s in range(1, n_z):
        own_z = tmap(jnp.add, own_z, send(plane, "seg_z", forward(n_z, s)))
    pieces = [own_z] + [
        send(own_z, "seg_y", [(i, (i + s) % n_y) for i in range(n_y)]) for s in range(1, n_y)
    ]
    order = (y - jnp.arange(n_y)) % n_y
    quarter = tmap(
        lambda *p: jnp.stack(p)[order].reshape(
            (-1,) + p[0].shape[1:]
        ),
        *pieces,
    )
    quarter = tmap(jnp.add, quarter, own_y)
    lo, hi = ordered(quarter, swap(quarter, "seg_x"), xh == 0)
    half = tmap(jnp.add, joined(lo, hi), own_x)
    lo, hi = ordered(half, swap(half, "frm"), core == 0)
    return tmap(jnp.add, joined(lo, hi), own_core)


def block_terms(phi_q, phi_k, values, span):
    rows, length, heads, dim = phi_q.shape
    count = length // span
    pq = phi_q.reshape(rows, count, span, heads, dim)
    pk = phi_k.reshape(rows, count, span, heads, dim)
    vv = values.reshape(rows, count, span, heads, dim)
    scores = jnp.einsum("rnihd,rnjhd->rnhij", pq, pk, preferred_element_type=jnp.float32)
    causal = jnp.arange(span)[:, None] >= jnp.arange(span)[None, :]
    scores = jnp.where(causal, scores, 0.0)
    den_local = jnp.sum(scores, axis=-1)
    weights = scores.astype(jnp.bfloat16)
    num_local = jnp.einsum("rnhij,rnjhd->rnihd", weights, vv, preferred_element_type=jnp.float32)
    kv_blocks = jnp.einsum("rnjhd,rnjhe->rnhde", pk, vv, preferred_element_type=jnp.float32)
    k_blocks = jnp.sum(pk, axis=2, dtype=jnp.float32)
    return (pq, num_local, den_local, kv_blocks, k_blocks)


def finish(pq, num_local, den_local, kv_blocks, k_blocks, prior_kv, prior_k):
    rows, count, span, heads, dim = pq.shape
    before_kv = jnp.cumsum(kv_blocks, axis=1) - kv_blocks + prior_kv[:, None]
    before_k = jnp.cumsum(k_blocks, axis=1) - k_blocks + prior_k[:, None]
    pq32 = pq.astype(jnp.float32)
    num = num_local + jnp.einsum(
        "rnihd,rnhde->rnihe", pq32, before_kv, precision=lax.Precision.HIGHEST
    )
    den = jnp.transpose(den_local, (0, 1, 3, 2)) + jnp.einsum(
        "rnihd,rnhd->rnih", pq32, before_k, precision=lax.Precision.HIGHEST
    )
    result = (num / den[..., None]).astype(jnp.bfloat16)
    return result.reshape(rows, count * span, heads * dim)


def split_qkv(qkv):
    phi_q = features(qkv[:, :, 0].astype(jnp.float32)).astype(jnp.bfloat16)
    phi_k = features(qkv[:, :, 1].astype(jnp.float32)).astype(jnp.bfloat16)
    return (phi_q, phi_k, qkv[:, :, 2])


def shards(frames_in, w_qkv, w_out):
    rows, tok_local, width = frames_in.shape
    head_dim = width // HEADS
    qkv = jnp.einsum("rtd,de->rte", frames_in, w_qkv, preferred_element_type=jnp.float32).astype(
        jnp.bfloat16
    )
    parts = qkv.reshape(rows, tok_local, 3, HEADS, head_dim)
    phi_q, phi_k, values = split_qkv(parts)
    pq, num_local, den_local, kv_blocks, k_blocks = block_terms(phi_q, phi_k, values, SPAN)
    total_kv = jnp.sum(kv_blocks, axis=1)[0]
    total_k = jnp.sum(k_blocks, axis=1)[0]
    dense = total_kv.reshape(HEADS, -1, 128)
    prior_kv, prior_k = entering((dense, total_k))
    prior_kv = prior_kv.reshape(total_kv.shape)
    heads_out = finish(
        pq, num_local, den_local, kv_blocks, k_blocks, prior_kv[None], prior_k[None]
    )
    return jnp.einsum("rtd,de->rte", heads_out, w_out, preferred_element_type=jnp.float32).astype(
        jnp.bfloat16
    )


def solution(mesh):
    sizes = [n for _, n in SEG_SPLIT]
    devices = mesh.devices.reshape(
        *sizes, mesh.shape["frm"], mesh.shape["rec"]
    )
    fine = Mesh(devices, tuple(name for name, _ in SEG_SPLIT) + ("frm", "rec"))
    in_specs = (P("rec", SCAN_AXES, None), P(), P())
    out_specs = P("rec", SCAN_AXES, None)
    return jax.shard_map(shards, mesh=fine, in_specs=in_specs, out_specs=out_specs, check_vma=False)
```

```python
import jax
import jax.numpy as jnp
from jax import lax
from jax.sharding import Mesh, PartitionSpec as P

HEADS = 16
SPAN = 256

SEG_SPLIT = (("seg_z", 8), ("seg_y", 4), ("seg_x", 2))
SCAN_AXES = ("seg_z", "seg_y", "seg_x", "frm")


def features(t):
    return jnp.where(t > 0.0, t + 1.0, jnp.exp(jnp.minimum(t, 0.0)))


def tmap(f, *trees):
    return jax.tree.map(f, *trees)


def send(tree, axis, pairs):
    return tmap(lambda t: lax.ppermute(t, axis, perm=pairs), tree)


def swap(tree, axis):
    return send(tree, axis, [(0, 1), (1, 0)])


def forward(n, s):
    return [(i, i + s) for i in range(n - s)]


def part(tree, index, count):
    def one(t):
        size = t.shape[0] // count
        return lax.dynamic_slice_in_dim(t, index * size, size, axis=0)

    return tmap(one, tree)


def ordered(mine, other, first):
    lo = tmap(lambda a, b: jnp.where(first, a, b), mine, other)
    hi = tmap(lambda a, b: jnp.where(first, b, a), mine, other)
    return lo, hi


def keep(tree, cond):
    return tmap(lambda a: jnp.where(cond, a, jnp.zeros_like(a)), tree)


def joined(lo, hi):
    return tmap(lambda a, b: jnp.concatenate([a, b], axis=0), lo, hi)


def entering(total):
    core = lax.axis_index("frm")
    xh = lax.axis_index("seg_x")
    y = lax.axis_index("seg_y")
    z = lax.axis_index("seg_z")
    n_y = lax.axis_size("seg_y")
    n_z = lax.axis_size("seg_z")
    lo, hi = ordered(total, swap(total, "frm"), core == 0)
    own_core = keep(lo, core == 1)
    chip = part(tmap(jnp.add, lo, hi), core, 2)
    lo, hi = ordered(chip, swap(chip, "seg_x"), xh == 0)
    own_x = keep(lo, xh == 1)
    row = part(tmap(jnp.add, lo, hi), xh, 2)
    own_y = tmap(jnp.zeros_like, row)
    plane = part(row, y, n_y)
    for s in range(1, n_y):
        came = send(row, "seg_y", [(i, (i + s) % n_y) for i in range(n_y)])
        own_y = tmap(lambda a, b: a + jnp.where(y >= s, b, jnp.zeros_like(b)), own_y, came)
        plane = tmap(jnp.add, plane, part(came, y, n_y))
    own_z = tmap(jnp.zeros_like, plane)
    for s in range(1, n_z):
        own_z = tmap(jnp.add, own_z, send(plane, "seg_z", forward(n_z, s)))
    pieces = [own_z] + [
        send(own_z, "seg_y", [(i, (i + s) % n_y) for i in range(n_y)]) for s in range(1, n_y)
    ]
    order = (y - jnp.arange(n_y)) % n_y
    quarter = tmap(
        lambda *p: jnp.stack(p)[order].reshape(
            (-1,) + p[0].shape[1:]
        ),
        *pieces,
    )
    quarter = tmap(jnp.add, quarter, own_y)
    lo, hi = ordered(quarter, swap(quarter, "seg_x"), xh == 0)
    half = tmap(jnp.add, joined(lo, hi), own_x)
    lo, hi = ordered(half, swap(half, "frm"), core == 0)
    return tmap(jnp.add, joined(lo, hi), own_core)


def block_terms(phi_q, phi_k, values, span):
    rows, length, heads, dim = phi_q.shape
    count = length // span
    pq = phi_q.reshape(rows, count, span, heads, dim)
    pk = phi_k.reshape(rows, count, span, heads, dim)
    vv = values.reshape(rows, count, span, heads, dim)
    scores = jnp.einsum("rnihd,rnjhd->rnhij", pq, pk, preferred_element_type=jnp.float32)
    causal = jnp.arange(span)[:, None] >= jnp.arange(span)[None, :]
    scores = jnp.where(causal, scores, 0.0)
    den_local = jnp.sum(scores, axis=-1)
    weights = scores.astype(jnp.bfloat16)
    num_local = jnp.einsum("rnhij,rnjhd->rnihd", weights, vv, preferred_element_type=jnp.float32)
    kv_blocks = jnp.einsum("rnjhd,rnjhe->rnhde", pk, vv, preferred_element_type=jnp.float32)
    k_blocks = jnp.sum(pk, axis=2, dtype=jnp.float32)
    return (pq, num_local, den_local, kv_blocks, k_blocks)


def finish(pq, num_local, den_local, kv_blocks, k_blocks, prior_kv, prior_k):
    rows, count, span, heads, dim = pq.shape
    before_kv = jnp.cumsum(kv_blocks, axis=1) - kv_blocks + prior_kv[:, None]
    before_k = jnp.cumsum(k_blocks, axis=1) - k_blocks + prior_k[:, None]
    pq32 = pq.astype(jnp.float32)
    num = num_local + jnp.einsum(
        "rnihd,rnhde->rnihe", pq32, before_kv, precision=lax.Precision.HIGHEST
    )
    den = jnp.transpose(den_local, (0, 1, 3, 2)) + jnp.einsum(
        "rnihd,rnhd->rnih", pq32, before_k, precision=lax.Precision.HIGHEST
    )
    result = (num / den[..., None]).astype(jnp.bfloat16)
    return result.reshape(rows, count * span, heads * dim)


def split_qkv(qkv):
    phi_q = features(qkv[:, :, 0].astype(jnp.float32)).astype(jnp.bfloat16)
    phi_k = features(qkv[:, :, 1].astype(jnp.float32)).astype(jnp.bfloat16)
    return (phi_q, phi_k, qkv[:, :, 2])


def shards(frames_in, w_qkv, w_out):
    rows, tok_local, width = frames_in.shape
    head_dim = width // HEADS
    qkv = jnp.einsum("rtd,de->rte", frames_in, w_qkv, preferred_element_type=jnp.float32).astype(
        jnp.bfloat16
    )
    parts = qkv.reshape(rows, tok_local, 3, HEADS, head_dim)
    phi_q, phi_k, values = split_qkv(parts)
    pq, num_local, den_local, kv_blocks, k_blocks = block_terms(phi_q, phi_k, values, SPAN)
    total_kv = jnp.sum(kv_blocks, axis=1)[0]
    total_k = jnp.sum(k_blocks, axis=1)[0]
    lanes = 128
    dense = total_kv.reshape(HEADS, -1, lanes)
    rows_kv = dense.shape[1]
    norm = jnp.pad(total_k, ((0, 0), (0, lanes - total_k.shape[1])))[:, None]
    prior = entering(jnp.concatenate([dense, norm], axis=1))
    prior_kv = prior[:, :rows_kv].reshape(total_kv.shape)
    prior_k = prior[:, rows_kv, : total_k.shape[1]]
    heads_out = finish(
        pq, num_local, den_local, kv_blocks, k_blocks, prior_kv[None], prior_k[None]
    )
    return jnp.einsum("rtd,de->rte", heads_out, w_out, preferred_element_type=jnp.float32).astype(
        jnp.bfloat16
    )


def solution(mesh):
    sizes = [n for _, n in SEG_SPLIT]
    devices = mesh.devices.reshape(
        *sizes, mesh.shape["frm"], mesh.shape["rec"]
    )
    fine = Mesh(devices, tuple(name for name, _ in SEG_SPLIT) + ("frm", "rec"))
    in_specs = (P("rec", SCAN_AXES, None), P(), P())
    out_specs = P("rec", SCAN_AXES, None)
    return jax.shard_map(shards, mesh=fine, in_specs=in_specs, out_specs=out_specs, check_vma=False)
```

```python
import jax
import jax.numpy as jnp
from jax import lax
from jax.sharding import Mesh, PartitionSpec as P

HEADS = 16
SPAN = 256

SEG_SPLIT = (("seg_z", 8), ("seg_y", 4), ("seg_x", 2))
SCAN_AXES = ("seg_z", "seg_y", "seg_x", "frm")


def features(t):
    return jnp.where(t > 0.0, t + 1.0, jnp.exp(jnp.minimum(t, 0.0)))


def tmap(f, *trees):
    return jax.tree.map(f, *trees)


def send(tree, axis, pairs):
    return tmap(lambda t: lax.ppermute(t, axis, perm=pairs), tree)


def swap(tree, axis):
    return send(tree, axis, [(0, 1), (1, 0)])


def forward(n, s):
    return [(i, i + s) for i in range(n - s)]


def part(tree, index, count):
    def one(t):
        size = t.shape[0] // count
        return lax.dynamic_slice_in_dim(t, index * size, size, axis=0)

    return tmap(one, tree)


def ordered(mine, other, first):
    lo = tmap(lambda a, b: jnp.where(first, a, b), mine, other)
    hi = tmap(lambda a, b: jnp.where(first, b, a), mine, other)
    return lo, hi


def keep(tree, cond):
    return tmap(lambda a: jnp.where(cond, a, jnp.zeros_like(a)), tree)


def joined(lo, hi):
    return tmap(lambda a, b: jnp.concatenate([a, b], axis=0), lo, hi)


def cyclic(n, s):
    return [(i, (i + s) % n) for i in range(n)]


def entering(total):
    core = lax.axis_index("frm")
    xh = lax.axis_index("seg_x")
    y = lax.axis_index("seg_y")
    n_y = lax.axis_size("seg_y")
    n_z = lax.axis_size("seg_z")
    add = lambda a, b: tmap(jnp.add, a, b)
    own_c = part(total, core, 2)
    got_c = swap(part(total, 1 - core, 2), "frm")
    lo, hi = ordered(own_c, got_c, core == 0)
    chip = add(lo, hi)
    own_x = part(chip, xh, 2)
    got_x = swap(part(chip, 1 - xh, 2), "seg_x")
    lo, hi = ordered(own_x, got_x, xh == 0)
    row = add(lo, hi)
    came = [part(row, y, n_y)] + [
        send(part(row, (y + s) % n_y, n_y), "seg_y", cyclic(n_y, s)) for s in range(1, n_y)
    ]
    plane = came[0]
    for c in came[1:]:
        plane = add(plane, c)
    upto = plane
    s = 1
    while s < n_z:
        upto = add(upto, send(upto, "seg_z", forward(n_z, s)))
        s *= 2
    before_z = tmap(jnp.subtract, upto, plane)

    def for_row(t):
        out = before_z
        for s, c in enumerate(came):
            out = add(out, keep(c, (y - s) % n_y < t))
        return out

    pieces = [for_row(y)] + [
        send(for_row((y + s) % n_y), "seg_y", cyclic(n_y, s)) for s in range(1, n_y)
    ]
    order = (y - jnp.arange(n_y)) % n_y
    quarter = tmap(
        lambda *p: jnp.stack(p)[order].reshape((-1,) + p[0].shape[1:]),
        *pieces,
    )
    got = swap(add(quarter, keep(own_x, xh == 0)), "seg_x")
    lo = tmap(lambda a, b: jnp.where(xh == 0, a, b), quarter, got)
    hi = tmap(lambda a, b, c: jnp.where(xh == 0, b, a + c), quarter, got, got_x)
    half = joined(lo, hi)
    got = swap(add(half, keep(own_c, core == 0)), "frm")
    lo = tmap(lambda a, b: jnp.where(core == 0, a, b), half, got)
    hi = tmap(lambda a, b, c: jnp.where(core == 0, b, a + c), half, got, got_c)
    return joined(lo, hi)


def block_terms(phi_q, phi_k, values, span):
    rows, length, heads, dim = phi_q.shape
    count = length // span
    pq = phi_q.reshape(rows, count, span, heads, dim)
    pk = phi_k.reshape(rows, count, span, heads, dim)
    vv = values.reshape(rows, count, span, heads, dim)
    scores = jnp.einsum("rnihd,rnjhd->rnhij", pq, pk, preferred_element_type=jnp.float32)
    causal = jnp.arange(span)[:, None] >= jnp.arange(span)[None, :]
    scores = jnp.where(causal, scores, 0.0)
    den_local = jnp.sum(scores, axis=-1)
    weights = scores.astype(jnp.bfloat16)
    num_local = jnp.einsum("rnhij,rnjhd->rnihd", weights, vv, preferred_element_type=jnp.float32)
    kv_blocks = jnp.einsum("rnjhd,rnjhe->rnhde", pk, vv, preferred_element_type=jnp.float32)
    k_blocks = jnp.sum(pk, axis=2, dtype=jnp.float32)
    return (pq, num_local, den_local, kv_blocks, k_blocks)


def finish(pq, num_local, den_local, kv_blocks, k_blocks, prior_kv, prior_k):
    rows, count, span, heads, dim = pq.shape
    before_kv = jnp.cumsum(kv_blocks, axis=1) - kv_blocks + prior_kv[:, None]
    before_k = jnp.cumsum(k_blocks, axis=1) - k_blocks + prior_k[:, None]
    pq32 = pq.astype(jnp.float32)
    num = num_local + jnp.einsum(
        "rnihd,rnhde->rnihe", pq32, before_kv, precision=lax.Precision.HIGHEST
    )
    den = jnp.transpose(den_local, (0, 1, 3, 2)) + jnp.einsum(
        "rnihd,rnhd->rnih", pq32, before_k, precision=lax.Precision.HIGHEST
    )
    result = (num / den[..., None]).astype(jnp.bfloat16)
    return result.reshape(rows, count * span, heads * dim)


def split_qkv(qkv):
    phi_q = features(qkv[:, :, 0].astype(jnp.float32)).astype(jnp.bfloat16)
    phi_k = features(qkv[:, :, 1].astype(jnp.float32)).astype(jnp.bfloat16)
    return (phi_q, phi_k, qkv[:, :, 2])


def shards(frames_in, w_qkv, w_out):
    rows, tok_local, width = frames_in.shape
    head_dim = width // HEADS
    qkv = jnp.einsum("rtd,de->rte", frames_in, w_qkv, preferred_element_type=jnp.float32).astype(
        jnp.bfloat16
    )
    parts = qkv.reshape(rows, tok_local, 3, HEADS, head_dim)
    phi_q, phi_k, values = split_qkv(parts)
    pq, num_local, den_local, kv_blocks, k_blocks = block_terms(phi_q, phi_k, values, SPAN)
    total_kv = jnp.sum(kv_blocks, axis=1)[0]
    total_k = jnp.sum(k_blocks, axis=1)[0]
    lanes = 128
    dense = total_kv.reshape(HEADS, -1, lanes)
    rows_kv = dense.shape[1]
    norm = jnp.pad(total_k, ((0, 0), (0, lanes - total_k.shape[1])))[:, None]
    prior = entering(jnp.concatenate([dense, norm], axis=1))
    prior_kv = prior[:, :rows_kv].reshape(total_kv.shape)
    prior_k = prior[:, rows_kv, : total_k.shape[1]]
    heads_out = finish(
        pq, num_local, den_local, kv_blocks, k_blocks, prior_kv[None], prior_k[None]
    )
    return jnp.einsum("rtd,de->rte", heads_out, w_out, preferred_element_type=jnp.float32).astype(
        jnp.bfloat16
    )


def solution(mesh):
    sizes = [n for _, n in SEG_SPLIT]
    devices = mesh.devices.reshape(
        *sizes, mesh.shape["frm"], mesh.shape["rec"]
    )
    fine = Mesh(devices, tuple(name for name, _ in SEG_SPLIT) + ("frm", "rec"))
    in_specs = (P("rec", SCAN_AXES, None), P(), P())
    out_specs = P("rec", SCAN_AXES, None)
    return jax.shard_map(shards, mesh=fine, in_specs=in_specs, out_specs=out_specs, check_vma=False)
```

```python
import jax
import jax.numpy as jnp
from jax import lax
from jax.sharding import Mesh, PartitionSpec as P

HEADS = 16
SPAN = 256

SEG_SPLIT = (("seg_z", 8), ("seg_y", 4), ("seg_x", 2))
SCAN_AXES = ("seg_z", "seg_y", "seg_x", "frm")


def features(t):
    return jnp.where(t > 0.0, t + 1.0, jnp.exp(jnp.minimum(t, 0.0)))


def tmap(f, *trees):
    return jax.tree.map(f, *trees)


def send(tree, axis, pairs):
    return tmap(lambda t: lax.ppermute(t, axis, perm=pairs), tree)


def swap(tree, axis):
    return send(tree, axis, [(0, 1), (1, 0)])


def forward(n, s):
    return [(i, i + s) for i in range(n - s)]


def part(tree, index, count):
    def one(t):
        size = t.shape[0] // count
        return lax.dynamic_slice_in_dim(t, index * size, size, axis=0)

    return tmap(one, tree)


def ordered(mine, other, first):
    lo = tmap(lambda a, b: jnp.where(first, a, b), mine, other)
    hi = tmap(lambda a, b: jnp.where(first, b, a), mine, other)
    return lo, hi


def keep(tree, cond):
    return tmap(lambda a: jnp.where(cond, a, jnp.zeros_like(a)), tree)


def joined(lo, hi):
    return tmap(lambda a, b: jnp.concatenate([a, b], axis=0), lo, hi)


def cyclic(n, s):
    return [(i, (i + s) % n) for i in range(n)]


def entering(total):
    core = lax.axis_index("frm")
    xh = lax.axis_index("seg_x")
    y = lax.axis_index("seg_y")
    z = lax.axis_index("seg_z")
    n_y = lax.axis_size("seg_y")
    n_z = lax.axis_size("seg_z")
    add = lambda a, b: tmap(jnp.add, a, b)
    own_c = part(total, core, 2)
    got_c = swap(part(total, 1 - core, 2), "frm")
    lo, hi = ordered(own_c, got_c, core == 0)
    chip = add(lo, hi)
    came = [part(chip, y, n_y)] + [
        send(part(chip, (y + s) % n_y, n_y), "seg_y", cyclic(n_y, s)) for s in range(1, n_y)
    ]
    column = came[0]
    for c in came[1:]:
        column = add(column, c)
    before_z = tmap(jnp.zeros_like, column)
    left = right = column
    for r in range(1, n_z // 2 + 1):
        left = send(left, "seg_z", cyclic(n_z, 1))
        before_z = add(before_z, keep(left, z >= r))
        if r < n_z - r:
            right = send(right, "seg_z", cyclic(n_z, -1))
            before_z = add(before_z, keep(right, z + r >= n_z))

    def for_row(t):
        out = before_z
        for s, c in enumerate(came):
            out = add(out, keep(c, (y - s) % n_y < t))
        return out

    pieces = [for_row(y)] + [
        send(for_row((y + s) % n_y), "seg_y", cyclic(n_y, s)) for s in range(1, n_y)
    ]
    order = (y - jnp.arange(n_y)) % n_y
    mine = tmap(
        lambda *p: jnp.stack(p)[order].reshape((-1,) + p[0].shape[1:]),
        *pieces,
    )
    half = add(mine, swap(add(mine, keep(chip, xh == 0)), "seg_x"))
    got = swap(add(half, keep(own_c, core == 0)), "frm")
    lo = tmap(lambda a, b: jnp.where(core == 0, a, b), half, got)
    hi = tmap(lambda a, b, c: jnp.where(core == 0, b, a + c), half, got, got_c)
    return joined(lo, hi)


def block_terms(phi_q, phi_k, values, span):
    rows, length, heads, dim = phi_q.shape
    count = length // span
    pq = phi_q.reshape(rows, count, span, heads, dim)
    pk = phi_k.reshape(rows, count, span, heads, dim)
    vv = values.reshape(rows, count, span, heads, dim)
    scores = jnp.einsum("rnihd,rnjhd->rnhij", pq, pk, preferred_element_type=jnp.float32)
    causal = jnp.arange(span)[:, None] >= jnp.arange(span)[None, :]
    scores = jnp.where(causal, scores, 0.0)
    den_local = jnp.sum(scores, axis=-1)
    weights = scores.astype(jnp.bfloat16)
    num_local = jnp.einsum("rnhij,rnjhd->rnihd", weights, vv, preferred_element_type=jnp.float32)
    kv_blocks = jnp.einsum("rnjhd,rnjhe->rnhde", pk, vv, preferred_element_type=jnp.float32)
    k_blocks = jnp.sum(pk, axis=2, dtype=jnp.float32)
    return (pq, num_local, den_local, kv_blocks, k_blocks)


def finish(pq, num_local, den_local, kv_blocks, k_blocks, prior_kv, prior_k):
    rows, count, span, heads, dim = pq.shape
    before_kv = jnp.cumsum(kv_blocks, axis=1) - kv_blocks + prior_kv[:, None]
    before_k = jnp.cumsum(k_blocks, axis=1) - k_blocks + prior_k[:, None]
    pq32 = pq.astype(jnp.float32)
    num = num_local + jnp.einsum(
        "rnihd,rnhde->rnihe", pq32, before_kv, precision=lax.Precision.HIGHEST
    )
    den = jnp.transpose(den_local, (0, 1, 3, 2)) + jnp.einsum(
        "rnihd,rnhd->rnih", pq32, before_k, precision=lax.Precision.HIGHEST
    )
    result = (num / den[..., None]).astype(jnp.bfloat16)
    return result.reshape(rows, count * span, heads * dim)


def split_qkv(qkv):
    phi_q = features(qkv[:, :, 0].astype(jnp.float32)).astype(jnp.bfloat16)
    phi_k = features(qkv[:, :, 1].astype(jnp.float32)).astype(jnp.bfloat16)
    return (phi_q, phi_k, qkv[:, :, 2])


def shards(frames_in, w_qkv, w_out):
    rows, tok_local, width = frames_in.shape
    head_dim = width // HEADS
    qkv = jnp.einsum("rtd,de->rte", frames_in, w_qkv, preferred_element_type=jnp.float32).astype(
        jnp.bfloat16
    )
    parts = qkv.reshape(rows, tok_local, 3, HEADS, head_dim)
    phi_q, phi_k, values = split_qkv(parts)
    pq, num_local, den_local, kv_blocks, k_blocks = block_terms(phi_q, phi_k, values, SPAN)
    total_kv = jnp.sum(kv_blocks, axis=1)[0]
    total_k = jnp.sum(k_blocks, axis=1)[0]
    lanes = 128
    dense = total_kv.reshape(HEADS, -1, lanes)
    rows_kv = dense.shape[1]
    norm = jnp.pad(total_k, ((0, 0), (0, lanes - total_k.shape[1])))[:, None]
    prior = entering(jnp.concatenate([dense, norm], axis=1))
    prior_kv = prior[:, :rows_kv].reshape(total_kv.shape)
    prior_k = prior[:, rows_kv, : total_k.shape[1]]
    heads_out = finish(
        pq, num_local, den_local, kv_blocks, k_blocks, prior_kv[None], prior_k[None]
    )
    return jnp.einsum("rtd,de->rte", heads_out, w_out, preferred_element_type=jnp.float32).astype(
        jnp.bfloat16
    )


def solution(mesh):
    sizes = [n for _, n in SEG_SPLIT]
    devices = mesh.devices.reshape(
        *sizes, mesh.shape["frm"], mesh.shape["rec"]
    )
    fine = Mesh(devices, tuple(name for name, _ in SEG_SPLIT) + ("frm", "rec"))
    in_specs = (P("rec", SCAN_AXES, None), P(), P())
    out_specs = P("rec", SCAN_AXES, None)
    return jax.shard_map(shards, mesh=fine, in_specs=in_specs, out_specs=out_specs, check_vma=False)
```

```python
import jax
import jax.numpy as jnp
from jax import lax
from jax.sharding import Mesh, PartitionSpec as P

HEADS = 16
SPAN = 256

SEG_SPLIT = (("seg_z", 8), ("seg_y", 4), ("seg_x", 2))
SCAN_AXES = ("seg_z", "seg_y", "seg_x", "frm")


def features(t):
    return jnp.where(t > 0.0, t + 1.0, jnp.exp(jnp.minimum(t, 0.0)))


def tmap(f, *trees):
    return jax.tree.map(f, *trees)


def send(tree, axis, pairs):
    return tmap(lambda t: lax.ppermute(t, axis, perm=pairs), tree)


def swap(tree, axis):
    return send(tree, axis, [(0, 1), (1, 0)])


def forward(n, s):
    return [(i, i + s) for i in range(n - s)]


def part(tree, index, count):
    def one(t):
        size = t.shape[0] // count
        return lax.dynamic_slice_in_dim(t, index * size, size, axis=0)

    return tmap(one, tree)


def ordered(mine, other, first):
    lo = tmap(lambda a, b: jnp.where(first, a, b), mine, other)
    hi = tmap(lambda a, b: jnp.where(first, b, a), mine, other)
    return lo, hi


def keep(tree, cond):
    return tmap(lambda a: jnp.where(cond, a, jnp.zeros_like(a)), tree)


def joined(lo, hi):
    return tmap(lambda a, b: jnp.concatenate([a, b], axis=0), lo, hi)


def cyclic(n, s):
    return [(i, (i + s) % n) for i in range(n)]


def entering(total):
    core = lax.axis_index("frm")
    xh = lax.axis_index("seg_x")
    y = lax.axis_index("seg_y")
    z = lax.axis_index("seg_z")
    n_y = lax.axis_size("seg_y")
    n_z = lax.axis_size("seg_z")
    add = lambda a, b: tmap(jnp.add, a, b)
    own_c = part(total, core, 2)
    got_c = swap(part(total, 1 - core, 2), "frm")
    lo, hi = ordered(own_c, got_c, core == 0)
    chip = add(lo, hi)
    came = lax.all_to_all(chip.reshape((n_y, -1) + chip.shape[1:]), "seg_y", 0, 0)
    column = jnp.sum(came, axis=0)
    later = lax.broadcasted_iota(jnp.int32, (n_z,) + column.shape, 0) > z
    before_z = lax.psum_scatter(jnp.where(later, column[None], 0.0), "seg_z", scatter_dimension=0)
    rows_before = jnp.cumsum(came, axis=0) - came
    mine = lax.all_to_all(before_z[None] + rows_before, "seg_y", 0, 0)
    mine = mine.reshape((-1,) + mine.shape[2:])
    half = add(mine, swap(add(mine, keep(chip, xh == 0)), "seg_x"))
    got = swap(add(half, keep(own_c, core == 0)), "frm")
    lo = tmap(lambda a, b: jnp.where(core == 0, a, b), half, got)
    hi = tmap(lambda a, b, c: jnp.where(core == 0, b, a + c), half, got, got_c)
    return joined(lo, hi)


def block_terms(phi_q, phi_k, values, span):
    rows, length, heads, dim = phi_q.shape
    count = length // span
    pq = phi_q.reshape(rows, count, span, heads, dim)
    pk = phi_k.reshape(rows, count, span, heads, dim)
    vv = values.reshape(rows, count, span, heads, dim)
    scores = jnp.einsum("rnihd,rnjhd->rnhij", pq, pk, preferred_element_type=jnp.float32)
    causal = jnp.arange(span)[:, None] >= jnp.arange(span)[None, :]
    scores = jnp.where(causal, scores, 0.0)
    den_local = jnp.sum(scores, axis=-1)
    weights = scores.astype(jnp.bfloat16)
    num_local = jnp.einsum("rnhij,rnjhd->rnihd", weights, vv, preferred_element_type=jnp.float32)
    kv_blocks = jnp.einsum("rnjhd,rnjhe->rnhde", pk, vv, preferred_element_type=jnp.float32)
    k_blocks = jnp.sum(pk, axis=2, dtype=jnp.float32)
    return (pq, num_local, den_local, kv_blocks, k_blocks)


def finish(pq, num_local, den_local, kv_blocks, k_blocks, prior_kv, prior_k):
    rows, count, span, heads, dim = pq.shape
    before_kv = jnp.cumsum(kv_blocks, axis=1) - kv_blocks + prior_kv[:, None]
    before_k = jnp.cumsum(k_blocks, axis=1) - k_blocks + prior_k[:, None]
    pq32 = pq.astype(jnp.float32)
    num = num_local + jnp.einsum(
        "rnihd,rnhde->rnihe", pq32, before_kv, precision=lax.Precision.HIGHEST
    )
    den = jnp.transpose(den_local, (0, 1, 3, 2)) + jnp.einsum(
        "rnihd,rnhd->rnih", pq32, before_k, precision=lax.Precision.HIGHEST
    )
    result = (num / den[..., None]).astype(jnp.bfloat16)
    return result.reshape(rows, count * span, heads * dim)


def split_qkv(qkv):
    phi_q = features(qkv[:, :, 0].astype(jnp.float32)).astype(jnp.bfloat16)
    phi_k = features(qkv[:, :, 1].astype(jnp.float32)).astype(jnp.bfloat16)
    return (phi_q, phi_k, qkv[:, :, 2])


def shards(frames_in, w_qkv, w_out):
    rows, tok_local, width = frames_in.shape
    head_dim = width // HEADS
    qkv = jnp.einsum("rtd,de->rte", frames_in, w_qkv, preferred_element_type=jnp.float32).astype(
        jnp.bfloat16
    )
    parts = qkv.reshape(rows, tok_local, 3, HEADS, head_dim)
    phi_q, phi_k, values = split_qkv(parts)
    pq, num_local, den_local, kv_blocks, k_blocks = block_terms(phi_q, phi_k, values, SPAN)
    total_kv = jnp.sum(kv_blocks, axis=1)[0]
    total_k = jnp.sum(k_blocks, axis=1)[0]
    lanes = 128
    dense = total_kv.reshape(HEADS, -1, lanes)
    rows_kv = dense.shape[1]
    norm = jnp.pad(total_k, ((0, 0), (0, lanes - total_k.shape[1])))[:, None]
    prior = entering(jnp.concatenate([dense, norm], axis=1))
    prior_kv = prior[:, :rows_kv].reshape(total_kv.shape)
    prior_k = prior[:, rows_kv, : total_k.shape[1]]
    heads_out = finish(
        pq, num_local, den_local, kv_blocks, k_blocks, prior_kv[None], prior_k[None]
    )
    return jnp.einsum("rtd,de->rte", heads_out, w_out, preferred_element_type=jnp.float32).astype(
        jnp.bfloat16
    )


def solution(mesh):
    sizes = [n for _, n in SEG_SPLIT]
    devices = mesh.devices.reshape(
        *sizes, mesh.shape["frm"], mesh.shape["rec"]
    )
    fine = Mesh(devices, tuple(name for name, _ in SEG_SPLIT) + ("frm", "rec"))
    in_specs = (P("rec", SCAN_AXES, None), P(), P())
    out_specs = P("rec", SCAN_AXES, None)
    return jax.shard_map(shards, mesh=fine, in_specs=in_specs, out_specs=out_specs, check_vma=False)
```

```python
import jax
import jax.numpy as jnp
from jax import lax
from jax.sharding import Mesh, PartitionSpec as P

HEADS = 16
SPAN = 256

SEG_SPLIT = (("seg_z", 8), ("seg_y", 4), ("seg_x", 2))
SCAN_AXES = ("seg_z", "seg_y", "seg_x", "frm")


def features(t):
    return jnp.where(t > 0.0, t + 1.0, jnp.exp(jnp.minimum(t, 0.0)))


def tmap(f, *trees):
    return jax.tree.map(f, *trees)


def send(tree, axis, pairs):
    return tmap(lambda t: lax.ppermute(t, axis, perm=pairs), tree)


def swap(tree, axis):
    return send(tree, axis, [(0, 1), (1, 0)])


def forward(n, s):
    return [(i, i + s) for i in range(n - s)]


def part(tree, index, count):
    def one(t):
        size = t.shape[0] // count
        return lax.dynamic_slice_in_dim(t, index * size, size, axis=0)

    return tmap(one, tree)


def ordered(mine, other, first):
    lo = tmap(lambda a, b: jnp.where(first, a, b), mine, other)
    hi = tmap(lambda a, b: jnp.where(first, b, a), mine, other)
    return lo, hi


def keep(tree, cond):
    return tmap(lambda a: jnp.where(cond, a, jnp.zeros_like(a)), tree)


def joined(lo, hi):
    return tmap(lambda a, b: jnp.concatenate([a, b], axis=0), lo, hi)


def cyclic(n, s):
    return [(i, (i + s) % n) for i in range(n)]


def entering(total, carry):
    core = lax.axis_index("frm")
    xh = lax.axis_index("seg_x")
    y = lax.axis_index("seg_y")
    z = lax.axis_index("seg_z")
    n_y = lax.axis_size("seg_y")
    n_z = lax.axis_size("seg_z")
    add = lambda a, b: tmap(jnp.add, a, b)
    own_c = part(total, core, 2)
    got_c = swap(part(total, 1 - core, 2), "frm")
    lo, hi = ordered(own_c, got_c, core == 0)
    chip = add(lo, hi)
    came = [part(chip, y, n_y)] + [
        send(part(chip, (y + s) % n_y, n_y), "seg_y", cyclic(n_y, s)) for s in range(1, n_y)
    ]
    column = came[0]
    for c in came[1:]:
        column = add(column, c)
    before_z = tmap(jnp.zeros_like, column)
    left = right = column
    for r in range(1, n_z // 2 + 1):
        left = send(left, "seg_z", cyclic(n_z, 1))
        before_z = add(before_z, keep(left, z >= r))
        if r < n_z - r:
            right = send(right, "seg_z", cyclic(n_z, -1))
            before_z = add(before_z, keep(right, z + r >= n_z))
    before_z, carry = lax.optimization_barrier((before_z, carry))

    def for_row(t):
        out = before_z
        for s, c in enumerate(came):
            out = add(out, keep(c, (y - s) % n_y < t))
        return out

    pieces = [for_row(y)] + [
        send(for_row((y + s) % n_y), "seg_y", cyclic(n_y, s)) for s in range(1, n_y)
    ]
    order = (y - jnp.arange(n_y)) % n_y
    mine = tmap(
        lambda *p: jnp.stack(p)[order].reshape((-1,) + p[0].shape[1:]),
        *pieces,
    )
    half = add(mine, swap(add(mine, keep(chip, xh == 0)), "seg_x"))
    got = swap(add(half, keep(own_c, core == 0)), "frm")
    lo = tmap(lambda a, b: jnp.where(core == 0, a, b), half, got)
    hi = tmap(lambda a, b, c: jnp.where(core == 0, b, a + c), half, got, got_c)
    return joined(lo, hi), carry


def block_terms(phi_q, phi_k, values, span):
    rows, length, heads, dim = phi_q.shape
    count = length // span
    pq = phi_q.reshape(rows, count, span, heads, dim)
    pk = phi_k.reshape(rows, count, span, heads, dim)
    vv = values.reshape(rows, count, span, heads, dim)
    scores = jnp.einsum("rnihd,rnjhd->rnhij", pq, pk, preferred_element_type=jnp.float32)
    causal = jnp.arange(span)[:, None] >= jnp.arange(span)[None, :]
    scores = jnp.where(causal, scores, 0.0)
    den_local = jnp.sum(scores, axis=-1)
    weights = scores.astype(jnp.bfloat16)
    num_local = jnp.einsum("rnhij,rnjhd->rnihd", weights, vv, preferred_element_type=jnp.float32)
    kv_blocks = jnp.einsum("rnjhd,rnjhe->rnhde", pk, vv, preferred_element_type=jnp.float32)
    k_blocks = jnp.sum(pk, axis=2, dtype=jnp.float32)
    return (pq, num_local, den_local, kv_blocks, k_blocks)


def finish(pq, num_local, den_local, kv_blocks, k_blocks, prior_kv, prior_k):
    rows, count, span, heads, dim = pq.shape
    before_kv = jnp.cumsum(kv_blocks, axis=1) - kv_blocks + prior_kv[:, None]
    before_k = jnp.cumsum(k_blocks, axis=1) - k_blocks + prior_k[:, None]
    pq32 = pq.astype(jnp.float32)
    num = num_local + jnp.einsum(
        "rnihd,rnhde->rnihe", pq32, before_kv, precision=lax.Precision.HIGHEST
    )
    den = jnp.transpose(den_local, (0, 1, 3, 2)) + jnp.einsum(
        "rnihd,rnhd->rnih", pq32, before_k, precision=lax.Precision.HIGHEST
    )
    result = (num / den[..., None]).astype(jnp.bfloat16)
    return result.reshape(rows, count * span, heads * dim)


def split_qkv(qkv):
    phi_q = features(qkv[:, :, 0].astype(jnp.float32)).astype(jnp.bfloat16)
    phi_k = features(qkv[:, :, 1].astype(jnp.float32)).astype(jnp.bfloat16)
    return (phi_q, phi_k, qkv[:, :, 2])


def shards(frames_in, w_qkv, w_out):
    rows, tok_local, width = frames_in.shape
    head_dim = width // HEADS
    qkv = jnp.einsum("rtd,de->rte", frames_in, w_qkv, preferred_element_type=jnp.float32).astype(
        jnp.bfloat16
    )
    parts = qkv.reshape(rows, tok_local, 3, HEADS, head_dim)
    phi_q, phi_k, values = split_qkv(parts)
    pq, num_local, den_local, kv_blocks, k_blocks = block_terms(phi_q, phi_k, values, SPAN)
    total_kv = jnp.sum(kv_blocks, axis=1)[0]
    total_k = jnp.sum(k_blocks, axis=1)[0]
    lanes = 128
    dense = total_kv.reshape(HEADS, -1, lanes)
    rows_kv = dense.shape[1]
    norm = jnp.pad(total_k, ((0, 0), (0, lanes - total_k.shape[1])))[:, None]
    prior, (num_local, den_local) = entering(
        jnp.concatenate([dense, norm], axis=1), (num_local, den_local)
    )
    prior_kv = prior[:, :rows_kv].reshape(total_kv.shape)
    prior_k = prior[:, rows_kv, : total_k.shape[1]]
    heads_out = finish(
        pq, num_local, den_local, kv_blocks, k_blocks, prior_kv[None], prior_k[None]
    )
    return jnp.einsum("rtd,de->rte", heads_out, w_out, preferred_element_type=jnp.float32).astype(
        jnp.bfloat16
    )


def solution(mesh):
    sizes = [n for _, n in SEG_SPLIT]
    devices = mesh.devices.reshape(
        *sizes, mesh.shape["frm"], mesh.shape["rec"]
    )
    fine = Mesh(devices, tuple(name for name, _ in SEG_SPLIT) + ("frm", "rec"))
    in_specs = (P("rec", SCAN_AXES, None), P(), P())
    out_specs = P("rec", SCAN_AXES, None)
    return jax.shard_map(shards, mesh=fine, in_specs=in_specs, out_specs=out_specs, check_vma=False)
```

```python
import jax
import jax.numpy as jnp
from jax import lax
from jax.sharding import Mesh, PartitionSpec as P

HEADS = 16
SPAN = 256

SEG_SPLIT = (("seg_z", 8), ("seg_y", 4), ("seg_x", 2))
SCAN_AXES = ("seg_z", "seg_y", "seg_x", "frm")


def features(t):
    return jnp.where(t > 0.0, t + 1.0, jnp.exp(jnp.minimum(t, 0.0)))


def tmap(f, *trees):
    return jax.tree.map(f, *trees)


def send(tree, axis, pairs):
    return tmap(lambda t: lax.ppermute(t, axis, perm=pairs), tree)


def swap(tree, axis):
    return send(tree, axis, [(0, 1), (1, 0)])


def forward(n, s):
    return [(i, i + s) for i in range(n - s)]


def part(tree, index, count):
    def one(t):
        size = t.shape[0] // count
        return lax.dynamic_slice_in_dim(t, index * size, size, axis=0)

    return tmap(one, tree)


def ordered(mine, other, first):
    lo = tmap(lambda a, b: jnp.where(first, a, b), mine, other)
    hi = tmap(lambda a, b: jnp.where(first, b, a), mine, other)
    return lo, hi


def keep(tree, cond):
    return tmap(lambda a: jnp.where(cond, a, jnp.zeros_like(a)), tree)


def joined(lo, hi):
    return tmap(lambda a, b: jnp.concatenate([a, b], axis=0), lo, hi)


def cyclic(n, s):
    return [(i, (i + s) % n) for i in range(n)]


def entering(total, carry):
    core = lax.axis_index("frm")
    xh = lax.axis_index("seg_x")
    y = lax.axis_index("seg_y")
    z = lax.axis_index("seg_z")
    n_y = lax.axis_size("seg_y")
    n_z = lax.axis_size("seg_z")
    add = lambda a, b: tmap(jnp.add, a, b)
    own_c = part(total, core, 2)
    got_c = swap(part(total, 1 - core, 2), "frm")
    lo, hi = ordered(own_c, got_c, core == 0)
    chip = add(lo, hi)
    came = [part(chip, y, n_y)] + [
        send(part(chip, (y + s) % n_y, n_y), "seg_y", cyclic(n_y, s)) for s in range(1, n_y)
    ]
    column = came[0]
    for c in came[1:]:
        column = add(column, c)
    before_z = tmap(jnp.zeros_like, column)
    left = right = column
    for r in range(1, n_z // 2 + 1):
        left = send(left, "seg_z", cyclic(n_z, 1))
        before_z = add(before_z, keep(left, z >= r))
        if r < n_z - r:
            right = send(right, "seg_z", cyclic(n_z, -1))
            before_z = add(before_z, keep(right, z + r >= n_z))
    before_z, carry = lax.optimization_barrier((before_z, carry))

    def for_row(t):
        out = before_z
        for s, c in enumerate(came):
            out = add(out, keep(c, (y - s) % n_y < t))
        return out

    pieces = [for_row(y)] + [
        send(for_row((y + s) % n_y), "seg_y", cyclic(n_y, s)) for s in range(1, n_y)
    ]
    order = (y - jnp.arange(n_y)) % n_y
    mine = tmap(
        lambda *p: jnp.stack(p)[order].reshape((-1,) + p[0].shape[1:]),
        *pieces,
    )
    half = add(mine, swap(add(mine, keep(chip, xh == 0)), "seg_x"))
    got = swap(add(half, keep(own_c, core == 0)), "frm")
    lo = tmap(lambda a, b: jnp.where(core == 0, a, b), half, got)
    hi = tmap(lambda a, b, c: jnp.where(core == 0, b, a + c), half, got, got_c)
    return joined(lo, hi), carry


def block_terms(phi_q, phi_k, values, span):
    rows, length, heads, dim = phi_q.shape
    count = length // span
    pq = phi_q.reshape(rows, count, span, heads, dim)
    pk = phi_k.reshape(rows, count, span, heads, dim)
    vv = values.reshape(rows, count, span, heads, dim)
    scores = jnp.einsum("rnihd,rnjhd->rnhij", pq, pk, preferred_element_type=jnp.float32)
    causal = jnp.arange(span)[:, None] >= jnp.arange(span)[None, :]
    scores = jnp.where(causal, scores, 0.0)
    den_local = jnp.sum(scores, axis=-1)
    weights = scores.astype(jnp.bfloat16)
    num_local = jnp.einsum("rnhij,rnjhd->rnihd", weights, vv, preferred_element_type=jnp.float32)
    kv_blocks = jnp.einsum("rnjhd,rnjhe->rnhde", pk, vv, preferred_element_type=jnp.float32)
    k_blocks = jnp.sum(pk, axis=2, dtype=jnp.float32)
    return (pq, num_local, den_local, kv_blocks, k_blocks)


def finish(pq, num_local, den_local, kv_blocks, k_blocks, prior_kv, prior_k):
    rows, count, span, heads, dim = pq.shape
    before_kv = jnp.cumsum(kv_blocks, axis=1) - kv_blocks + prior_kv[:, None]
    before_k = jnp.cumsum(k_blocks, axis=1) - k_blocks + prior_k[:, None]
    pq32 = pq.astype(jnp.float32)
    num = num_local + jnp.einsum(
        "rnihd,rnhde->rnihe", pq32, before_kv, precision=lax.Precision.HIGHEST
    )
    den = jnp.transpose(den_local, (0, 1, 3, 2)) + jnp.einsum(
        "rnihd,rnhd->rnih", pq32, before_k, precision=lax.Precision.HIGHEST
    )
    result = (num / den[..., None]).astype(jnp.bfloat16)
    return result.reshape(rows, count * span, heads * dim)


def split_qkv(qkv):
    phi_q = features(qkv[:, :, 0].astype(jnp.float32)).astype(jnp.bfloat16)
    phi_k = features(qkv[:, :, 1].astype(jnp.float32)).astype(jnp.bfloat16)
    return (phi_q, phi_k, qkv[:, :, 2])


def shards(frames_in, w_qkv, w_out):
    rows, tok_local, width = frames_in.shape
    head_dim = width // HEADS
    qkv = jnp.einsum("rtd,de->ret", frames_in, w_qkv, preferred_element_type=jnp.float32).astype(
        jnp.bfloat16
    )
    parts = jnp.transpose(qkv.reshape(rows, 3, HEADS, head_dim, tok_local), (0, 4, 1, 2, 3))
    phi_q, phi_k, values = split_qkv(parts)
    pq, num_local, den_local, kv_blocks, k_blocks = block_terms(phi_q, phi_k, values, SPAN)
    total_kv = jnp.sum(kv_blocks, axis=1)[0]
    total_k = jnp.sum(k_blocks, axis=1)[0]
    lanes = 128
    dense = total_kv.reshape(HEADS, -1, lanes)
    rows_kv = dense.shape[1]
    norm = jnp.pad(total_k, ((0, 0), (0, lanes - total_k.shape[1])))[:, None]
    prior, (num_local, den_local) = entering(
        jnp.concatenate([dense, norm], axis=1), (num_local, den_local)
    )
    prior_kv = prior[:, :rows_kv].reshape(total_kv.shape)
    prior_k = prior[:, rows_kv, : total_k.shape[1]]
    heads_out = finish(
        pq, num_local, den_local, kv_blocks, k_blocks, prior_kv[None], prior_k[None]
    )
    return jnp.einsum("rtd,de->rte", heads_out, w_out, preferred_element_type=jnp.float32).astype(
        jnp.bfloat16
    )


def solution(mesh):
    sizes = [n for _, n in SEG_SPLIT]
    devices = mesh.devices.reshape(
        *sizes, mesh.shape["frm"], mesh.shape["rec"]
    )
    fine = Mesh(devices, tuple(name for name, _ in SEG_SPLIT) + ("frm", "rec"))
    in_specs = (P("rec", SCAN_AXES, None), P(), P())
    out_specs = P("rec", SCAN_AXES, None)
    return jax.shard_map(shards, mesh=fine, in_specs=in_specs, out_specs=out_specs, check_vma=False)
```

```python
import jax
import jax.numpy as jnp
from jax import lax
from jax.sharding import Mesh, PartitionSpec as P

HEADS = 16
SPAN = 256

SEG_SPLIT = (("seg_z", 8), ("seg_y", 4), ("seg_x", 2))
SCAN_AXES = ("seg_z", "seg_y", "seg_x", "frm")


def features(t):
    return jnp.where(t > 0.0, t + 1.0, jnp.exp(jnp.minimum(t, 0.0)))


def tmap(f, *trees):
    return jax.tree.map(f, *trees)


def send(tree, axis, pairs):
    return tmap(lambda t: lax.ppermute(t, axis, perm=pairs), tree)


def swap(tree, axis):
    return send(tree, axis, [(0, 1), (1, 0)])


def forward(n, s):
    return [(i, i + s) for i in range(n - s)]


def part(tree, index, count):
    def one(t):
        size = t.shape[0] // count
        return lax.dynamic_slice_in_dim(t, index * size, size, axis=0)

    return tmap(one, tree)


def ordered(mine, other, first):
    lo = tmap(lambda a, b: jnp.where(first, a, b), mine, other)
    hi = tmap(lambda a, b: jnp.where(first, b, a), mine, other)
    return lo, hi


def keep(tree, cond):
    return tmap(lambda a: jnp.where(cond, a, jnp.zeros_like(a)), tree)


def joined(lo, hi):
    return tmap(lambda a, b: jnp.concatenate([a, b], axis=0), lo, hi)


def cyclic(n, s):
    return [(i, (i + s) % n) for i in range(n)]


def entering(total, carry):
    core = lax.axis_index("frm")
    xh = lax.axis_index("seg_x")
    y = lax.axis_index("seg_y")
    z = lax.axis_index("seg_z")
    n_y = lax.axis_size("seg_y")
    n_z = lax.axis_size("seg_z")
    add = lambda a, b: tmap(jnp.add, a, b)
    own_c = part(total, core, 2)
    got_c = swap(part(total, 1 - core, 2), "frm")
    lo, hi = ordered(own_c, got_c, core == 0)
    chip = add(lo, hi)
    came = [part(chip, y, n_y)] + [
        send(part(chip, (y + s) % n_y, n_y), "seg_y", cyclic(n_y, s)) for s in range(1, n_y)
    ]
    column = came[0]
    for c in came[1:]:
        column = add(column, c)
    lo, hi = ordered(column, swap(column, "frm"), core == 0)
    both = joined(lo, hi)
    ring = [(z_ * 2, ((z_ + 1) % n_z) * 2) for z_ in range(n_z)]
    ring += [(z_ * 2 + 1, ((z_ - 1) % n_z) * 2 + 1) for z_ in range(n_z)]
    stream = tmap(jnp.zeros_like, both)
    piece = both
    for r in range(1, n_z // 2 + 1):
        piece = send(piece, ("seg_z", "frm"), ring)
        early = jnp.where(core == 0, z >= r, (z + r >= n_z) & (r < n_z - r))
        stream = add(stream, keep(piece, early))
    before_z = add(part(stream, core, 2), swap(part(stream, 1 - core, 2), "frm"))
    before_z, carry = lax.optimization_barrier((before_z, carry))

    def for_row(t):
        out = before_z
        for s, c in enumerate(came):
            out = add(out, keep(c, (y - s) % n_y < t))
        return out

    pieces = [for_row(y)] + [
        send(for_row((y + s) % n_y), "seg_y", cyclic(n_y, s)) for s in range(1, n_y)
    ]
    order = (y - jnp.arange(n_y)) % n_y
    mine = tmap(
        lambda *p: jnp.stack(p)[order].reshape((-1,) + p[0].shape[1:]),
        *pieces,
    )
    half = add(mine, swap(add(mine, keep(chip, xh == 0)), "seg_x"))
    got = swap(add(half, keep(own_c, core == 0)), "frm")
    lo = tmap(lambda a, b: jnp.where(core == 0, a, b), half, got)
    hi = tmap(lambda a, b, c: jnp.where(core == 0, b, a + c), half, got, got_c)
    return joined(lo, hi), carry


def block_terms(phi_q, phi_k, values, span):
    rows, length, heads, dim = phi_q.shape
    count = length // span
    pq = phi_q.reshape(rows, count, span, heads, dim)
    pk = phi_k.reshape(rows, count, span, heads, dim)
    vv = values.reshape(rows, count, span, heads, dim)
    scores = jnp.einsum("rnihd,rnjhd->rnhij", pq, pk, preferred_element_type=jnp.float32)
    causal = jnp.arange(span)[:, None] >= jnp.arange(span)[None, :]
    scores = jnp.where(causal, scores, 0.0)
    den_local = jnp.sum(scores, axis=-1)
    weights = scores.astype(jnp.bfloat16)
    num_local = jnp.einsum("rnhij,rnjhd->rnihd", weights, vv, preferred_element_type=jnp.float32)
    kv_blocks = jnp.einsum("rnjhd,rnjhe->rnhde", pk, vv, preferred_element_type=jnp.float32)
    k_blocks = jnp.sum(pk, axis=2, dtype=jnp.float32)
    return (pq, num_local, den_local, kv_blocks, k_blocks)


def finish(pq, num_local, den_local, kv_blocks, k_blocks, prior_kv, prior_k):
    rows, count, span, heads, dim = pq.shape
    before_kv = jnp.cumsum(kv_blocks, axis=1) - kv_blocks + prior_kv[:, None]
    before_k = jnp.cumsum(k_blocks, axis=1) - k_blocks + prior_k[:, None]
    pq32 = pq.astype(jnp.float32)
    num = num_local + jnp.einsum(
        "rnihd,rnhde->rnihe", pq32, before_kv, precision=lax.Precision.HIGHEST
    )
    den = jnp.transpose(den_local, (0, 1, 3, 2)) + jnp.einsum(
        "rnihd,rnhd->rnih", pq32, before_k, precision=lax.Precision.HIGHEST
    )
    result = (num / den[..., None]).astype(jnp.bfloat16)
    return result.reshape(rows, count * span, heads * dim)


def split_qkv(qkv):
    phi_q = features(qkv[:, :, 0].astype(jnp.float32)).astype(jnp.bfloat16)
    phi_k = features(qkv[:, :, 1].astype(jnp.float32)).astype(jnp.bfloat16)
    return (phi_q, phi_k, qkv[:, :, 2])


def shards(frames_in, w_qkv, w_out):
    rows, tok_local, width = frames_in.shape
    head_dim = width // HEADS
    qkv = jnp.einsum("rtd,de->ret", frames_in, w_qkv, preferred_element_type=jnp.float32).astype(
        jnp.bfloat16
    )
    parts = jnp.transpose(qkv.reshape(rows, 3, HEADS, head_dim, tok_local), (0, 4, 1, 2, 3))
    phi_q, phi_k, values = split_qkv(parts)
    pq, num_local, den_local, kv_blocks, k_blocks = block_terms(phi_q, phi_k, values, SPAN)
    total_kv = jnp.sum(kv_blocks, axis=1)[0]
    total_k = jnp.sum(k_blocks, axis=1)[0]
    lanes = 128
    dense = total_kv.reshape(HEADS, -1, lanes)
    rows_kv = dense.shape[1]
    norm = jnp.pad(total_k, ((0, 0), (0, lanes - total_k.shape[1])))[:, None]
    prior, (num_local, den_local) = entering(
        jnp.concatenate([dense, norm], axis=1), (num_local, den_local)
    )
    prior_kv = prior[:, :rows_kv].reshape(total_kv.shape)
    prior_k = prior[:, rows_kv, : total_k.shape[1]]
    heads_out = finish(
        pq, num_local, den_local, kv_blocks, k_blocks, prior_kv[None], prior_k[None]
    )
    return jnp.einsum("rtd,de->rte", heads_out, w_out, preferred_element_type=jnp.float32).astype(
        jnp.bfloat16
    )


def solution(mesh):
    sizes = [n for _, n in SEG_SPLIT]
    devices = mesh.devices.reshape(
        *sizes, mesh.shape["frm"], mesh.shape["rec"]
    )
    fine = Mesh(devices, tuple(name for name, _ in SEG_SPLIT) + ("frm", "rec"))
    in_specs = (P("rec", SCAN_AXES, None), P(), P())
    out_specs = P("rec", SCAN_AXES, None)
    return jax.shard_map(shards, mesh=fine, in_specs=in_specs, out_specs=out_specs, check_vma=False)
```

```python
import jax
import jax.numpy as jnp
from jax import lax
from jax.sharding import Mesh, PartitionSpec as P

HEADS = 16
SPAN = 256

SEG_SPLIT = (("seg_z", 8), ("seg_y", 4), ("seg_x", 2))
SCAN_AXES = ("seg_z", "seg_y", "seg_x", "frm")


def features(t):
    return jnp.where(t > 0.0, t + 1.0, jnp.exp(jnp.minimum(t, 0.0)))


def tmap(f, *trees):
    return jax.tree.map(f, *trees)


def send(tree, axis, pairs):
    return tmap(lambda t: lax.ppermute(t, axis, perm=pairs), tree)


def swap(tree, axis):
    return send(tree, axis, [(0, 1), (1, 0)])


def forward(n, s):
    return [(i, i + s) for i in range(n - s)]


def part(tree, index, count):
    def one(t):
        size = t.shape[0] // count
        return lax.dynamic_slice_in_dim(t, index * size, size, axis=0)

    return tmap(one, tree)


def ordered(mine, other, first):
    lo = tmap(lambda a, b: jnp.where(first, a, b), mine, other)
    hi = tmap(lambda a, b: jnp.where(first, b, a), mine, other)
    return lo, hi


def keep(tree, cond):
    return tmap(lambda a: jnp.where(cond, a, jnp.zeros_like(a)), tree)


def joined(lo, hi):
    return tmap(lambda a, b: jnp.concatenate([a, b], axis=0), lo, hi)


def cyclic(n, s):
    return [(i, (i + s) % n) for i in range(n)]


def entering(total, carry):
    core = lax.axis_index("frm")
    xh = lax.axis_index("seg_x")
    y = lax.axis_index("seg_y")
    z = lax.axis_index("seg_z")
    n_y = lax.axis_size("seg_y")
    n_z = lax.axis_size("seg_z")
    add = lambda a, b: tmap(jnp.add, a, b)
    own_c = part(total, core, 2)
    got_c = swap(part(total, 1 - core, 2), "frm")
    lo, hi = ordered(own_c, got_c, core == 0)
    chip = add(lo, hi)
    came = [part(chip, y, n_y)] + [
        send(part(chip, (y + s) % n_y, n_y), "seg_y", cyclic(n_y, s)) for s in range(1, n_y)
    ]
    column = came[0]
    for c in came[1:]:
        column = add(column, c)
    before_z = tmap(jnp.zeros_like, column)
    left = right = column
    for r in range(1, n_z // 2 + 1):
        left = send(left, "seg_z", cyclic(n_z, 1))
        before_z = add(before_z, keep(left, z >= r))
        if r < n_z - r:
            right = send(right, "seg_z", cyclic(n_z, -1))
            before_z = add(before_z, keep(right, z + r >= n_z))
    before_z, carry = lax.optimization_barrier((before_z, carry))

    def for_row(t):
        out = before_z
        for s, c in enumerate(came):
            out = add(out, keep(c, (y - s) % n_y < t))
        return out

    pieces = [for_row(y)] + [
        send(for_row((y + s) % n_y), "seg_y", cyclic(n_y, s)) for s in range(1, n_y)
    ]
    order = (y - jnp.arange(n_y)) % n_y
    mine = tmap(
        lambda *p: jnp.stack(p)[order].reshape((-1,) + p[0].shape[1:]),
        *pieces,
    )
    half = add(mine, swap(add(mine, keep(chip, xh == 0)), "seg_x"))
    got = swap(add(half, keep(own_c, core == 0)), "frm")
    lo = tmap(lambda a, b: jnp.where(core == 0, a, b), half, got)
    hi = tmap(lambda a, b, c: jnp.where(core == 0, b, a + c), half, got, got_c)
    return joined(lo, hi), carry


def block_terms(phi_q, phi_k, values, span):
    rows, length, heads, dim = phi_q.shape
    count = length // span
    pq = phi_q.reshape(rows, count, span, heads, dim)
    pk = phi_k.reshape(rows, count, span, heads, dim)
    vv = values.reshape(rows, count, span, heads, dim)
    scores = jnp.einsum("rnihd,rnjhd->rnhij", pq, pk, preferred_element_type=jnp.float32)
    causal = jnp.arange(span)[:, None] >= jnp.arange(span)[None, :]
    scores = jnp.where(causal, scores, 0.0)
    den_local = jnp.sum(scores, axis=-1)
    weights = scores.astype(jnp.bfloat16)
    num_local = jnp.einsum("rnhij,rnjhd->rnihd", weights, vv, preferred_element_type=jnp.float32)
    kv_blocks = jnp.einsum("rnjhd,rnjhe->rnhde", pk, vv, preferred_element_type=jnp.float32)
    k_blocks = jnp.sum(pk, axis=2, dtype=jnp.float32)
    return (pq, num_local, den_local, kv_blocks, k_blocks)


def finish(pq, num_local, den_local, kv_blocks, k_blocks, prior_kv, prior_k):
    rows, count, span, heads, dim = pq.shape
    before_kv = jnp.cumsum(kv_blocks, axis=1) - kv_blocks + prior_kv[:, None]
    before_k = jnp.cumsum(k_blocks, axis=1) - k_blocks + prior_k[:, None]
    pq32 = pq.astype(jnp.float32)
    num = num_local + jnp.einsum(
        "rnihd,rnhde->rnihe", pq32, before_kv, precision=lax.Precision.HIGHEST
    )
    den = jnp.transpose(den_local, (0, 1, 3, 2)) + jnp.einsum(
        "rnihd,rnhd->rnih", pq32, before_k, precision=lax.Precision.HIGHEST
    )
    result = (num / den[..., None]).astype(jnp.bfloat16)
    return result.reshape(rows, count * span, heads * dim)


def split_qkv(qkv):
    phi_q = features(qkv[:, :, 0].astype(jnp.float32)).astype(jnp.bfloat16)
    phi_k = features(qkv[:, :, 1].astype(jnp.float32)).astype(jnp.bfloat16)
    return (phi_q, phi_k, qkv[:, :, 2])


def shards(frames_in, w_qkv, w_out):
    rows, tok_local, width = frames_in.shape
    head_dim = width // HEADS
    def project(w, count):
        out = jnp.einsum("rtd,de->ret", frames_in, w, preferred_element_type=jnp.float32)
        out = out.astype(jnp.bfloat16).reshape(rows, count, HEADS, head_dim, tok_local)
        return jnp.transpose(out, (0, 4, 1, 2, 3))

    keys_values = project(w_qkv[:, width:], 2)
    queries = project(w_qkv[:, :width], 1)
    phi_q = features(queries[:, :, 0].astype(jnp.float32)).astype(jnp.bfloat16)
    phi_k = features(keys_values[:, :, 0].astype(jnp.float32)).astype(jnp.bfloat16)
    values = keys_values[:, :, 1]
    pq, num_local, den_local, kv_blocks, k_blocks = block_terms(phi_q, phi_k, values, SPAN)
    total_kv = jnp.sum(kv_blocks, axis=1)[0]
    total_k = jnp.sum(k_blocks, axis=1)[0]
    lanes = 128
    dense = total_kv.reshape(HEADS, -1, lanes)
    rows_kv = dense.shape[1]
    norm = jnp.pad(total_k, ((0, 0), (0, lanes - total_k.shape[1])))[:, None]
    prior, (num_local, den_local) = entering(
        jnp.concatenate([dense, norm], axis=1), (num_local, den_local)
    )
    prior_kv = prior[:, :rows_kv].reshape(total_kv.shape)
    prior_k = prior[:, rows_kv, : total_k.shape[1]]
    heads_out = finish(
        pq, num_local, den_local, kv_blocks, k_blocks, prior_kv[None], prior_k[None]
    )
    return jnp.einsum("rtd,de->rte", heads_out, w_out, preferred_element_type=jnp.float32).astype(
        jnp.bfloat16
    )


def solution(mesh):
    sizes = [n for _, n in SEG_SPLIT]
    devices = mesh.devices.reshape(
        *sizes, mesh.shape["frm"], mesh.shape["rec"]
    )
    fine = Mesh(devices, tuple(name for name, _ in SEG_SPLIT) + ("frm", "rec"))
    in_specs = (P("rec", SCAN_AXES, None), P(), P())
    out_specs = P("rec", SCAN_AXES, None)
    return jax.shard_map(shards, mesh=fine, in_specs=in_specs, out_specs=out_specs, check_vma=False)
```

```python
import jax
import jax.numpy as jnp
from jax import lax
from jax.sharding import Mesh, PartitionSpec as P

HEADS = 16
SPAN = 256

SEG_SPLIT = (("seg_z", 8), ("seg_y", 4), ("seg_x", 2))
SCAN_AXES = ("seg_z", "seg_y", "seg_x", "frm")


def features(t):
    return jnp.where(t > 0.0, t + 1.0, jnp.exp(jnp.minimum(t, 0.0)))


def tmap(f, *trees):
    return jax.tree.map(f, *trees)


def send(tree, axis, pairs):
    return tmap(lambda t: lax.ppermute(t, axis, perm=pairs), tree)


def swap(tree, axis):
    return send(tree, axis, [(0, 1), (1, 0)])


def forward(n, s):
    return [(i, i + s) for i in range(n - s)]


def part(tree, index, count):
    def one(t):
        size = t.shape[0] // count
        return lax.dynamic_slice_in_dim(t, index * size, size, axis=0)

    return tmap(one, tree)


def ordered(mine, other, first):
    lo = tmap(lambda a, b: jnp.where(first, a, b), mine, other)
    hi = tmap(lambda a, b: jnp.where(first, b, a), mine, other)
    return lo, hi


def keep(tree, cond):
    return tmap(lambda a: jnp.where(cond, a, jnp.zeros_like(a)), tree)


def joined(lo, hi):
    return tmap(lambda a, b: jnp.concatenate([a, b], axis=0), lo, hi)


def cyclic(n, s):
    return [(i, (i + s) % n) for i in range(n)]


def entering(total, carry):
    core = lax.axis_index("frm")
    xh = lax.axis_index("seg_x")
    y = lax.axis_index("seg_y")
    z = lax.axis_index("seg_z")
    n_y = lax.axis_size("seg_y")
    n_z = lax.axis_size("seg_z")
    add = lambda a, b: tmap(jnp.add, a, b)
    own_c = part(total, core, 2)
    got_c = swap(part(total, 1 - core, 2), "frm")
    lo, hi = ordered(own_c, got_c, core == 0)
    chip = add(lo, hi)
    came = [part(chip, y, n_y)] + [
        send(part(chip, (y + s) % n_y, n_y), "seg_y", cyclic(n_y, s)) for s in range(1, n_y)
    ]
    column = came[0]
    for c in came[1:]:
        column = add(column, c)
    before_z = tmap(jnp.zeros_like, column)
    left = right = column
    for r in range(1, n_z // 2 + 1):
        left = send(left, "seg_z", cyclic(n_z, 1))
        before_z = add(before_z, keep(left, z >= r))
        if r < n_z - r:
            right = send(right, "seg_z", cyclic(n_z, -1))
            before_z = add(before_z, keep(right, z + r >= n_z))
    before_z, carry = lax.optimization_barrier((before_z, carry))

    def for_row(t):
        out = before_z
        for s, c in enumerate(came):
            out = add(out, keep(c, (y - s) % n_y < t))
        return out

    pieces = [for_row(y)] + [
        send(for_row((y + s) % n_y), "seg_y", cyclic(n_y, s)) for s in range(1, n_y)
    ]
    order = (y - jnp.arange(n_y)) % n_y
    mine = tmap(
        lambda *p: jnp.stack(p)[order].reshape((-1,) + p[0].shape[1:]),
        *pieces,
    )
    half = add(mine, swap(add(mine, keep(chip, xh == 0)), "seg_x"))
    got = swap(add(half, keep(own_c, core == 0)), "frm")
    own = tmap(lambda a, c: jnp.where(core == 0, a, a + c), half, got_c)
    return (own, got), carry


def block_terms(phi_q, phi_k, values, span):
    rows, length, heads, dim = phi_q.shape
    count = length // span
    pq = phi_q.reshape(rows, count, span, heads, dim)
    pk = phi_k.reshape(rows, count, span, heads, dim)
    vv = values.reshape(rows, count, span, heads, dim)
    scores = jnp.einsum("rnihd,rnjhd->rnhij", pq, pk, preferred_element_type=jnp.float32)
    causal = jnp.arange(span)[:, None] >= jnp.arange(span)[None, :]
    scores = jnp.where(causal, scores, 0.0)
    den_local = jnp.sum(scores, axis=-1)
    weights = scores.astype(jnp.bfloat16)
    num_local = jnp.einsum("rnhij,rnjhd->rnihd", weights, vv, preferred_element_type=jnp.float32)
    kv_blocks = jnp.einsum("rnjhd,rnjhe->rnhde", pk, vv, preferred_element_type=jnp.float32)
    k_blocks = jnp.sum(pk, axis=2, dtype=jnp.float32)
    return (pq, num_local, den_local, kv_blocks, k_blocks)


def finish(pq, num_local, den_local, kv_blocks, k_blocks, prior_kv, prior_k):
    rows, count, span, heads, dim = pq.shape
    before_kv = jnp.cumsum(kv_blocks, axis=1) - kv_blocks + prior_kv[:, None]
    before_k = jnp.cumsum(k_blocks, axis=1) - k_blocks + prior_k[:, None]
    pq32 = pq.astype(jnp.float32)
    num = num_local + jnp.einsum(
        "rnihd,rnhde->rnihe", pq32, before_kv, precision=lax.Precision.HIGHEST
    )
    den = jnp.transpose(den_local, (0, 1, 3, 2)) + jnp.einsum(
        "rnihd,rnhd->rnih", pq32, before_k, precision=lax.Precision.HIGHEST
    )
    result = (num / den[..., None]).astype(jnp.bfloat16)
    return result.reshape(rows, count * span, heads * dim)


def split_qkv(qkv):
    phi_q = features(qkv[:, :, 0].astype(jnp.float32)).astype(jnp.bfloat16)
    phi_k = features(qkv[:, :, 1].astype(jnp.float32)).astype(jnp.bfloat16)
    return (phi_q, phi_k, qkv[:, :, 2])


def shards(frames_in, w_qkv, w_out):
    rows, tok_local, width = frames_in.shape
    head_dim = width // HEADS
    def project(w, count):
        out = jnp.einsum("rtd,de->ret", frames_in, w, preferred_element_type=jnp.float32)
        out = out.astype(jnp.bfloat16).reshape(rows, count, HEADS, head_dim, tok_local)
        return jnp.transpose(out, (0, 4, 1, 2, 3))

    keys_values = project(w_qkv[:, width:], 2)
    queries = project(w_qkv[:, :width], 1)
    phi_q = features(queries[:, :, 0].astype(jnp.float32)).astype(jnp.bfloat16)
    phi_k = features(keys_values[:, :, 0].astype(jnp.float32)).astype(jnp.bfloat16)
    values = keys_values[:, :, 1]
    pq, num_local, den_local, kv_blocks, k_blocks = block_terms(phi_q, phi_k, values, SPAN)
    total_kv = jnp.sum(kv_blocks, axis=1)[0]
    total_k = jnp.sum(k_blocks, axis=1)[0]
    lanes = 128
    dense = total_kv.reshape(HEADS, -1, lanes)
    rows_kv = dense.shape[1]
    norm = jnp.pad(total_k, ((0, 0), (0, lanes - total_k.shape[1])))[:, None]
    (own, other), (num_local, den_local) = entering(
        jnp.concatenate([dense, norm], axis=1), (num_local, den_local)
    )
    core = lax.axis_index("frm")
    half_heads = HEADS // 2

    def heads_of(prior, which):
        first = which * half_heads
        pick = lambda t, axis: lax.dynamic_slice_in_dim(t, first, half_heads, axis=axis)
        prior_kv = prior[:, :rows_kv].reshape((half_heads,) + total_kv.shape[1:])
        prior_k = prior[:, rows_kv, : total_k.shape[1]]
        heads_out = finish(
            pick(pq, 3), pick(num_local, 3), pick(den_local, 2),
            pick(kv_blocks, 2), pick(k_blocks, 2), prior_kv[None], prior_k[None],
        )
        rows_w = lax.dynamic_slice_in_dim(w_out, first * head_dim, half_heads * head_dim, axis=0)
        return jnp.einsum("rtd,de->rte", heads_out, rows_w, preferred_element_type=jnp.float32)

    out = heads_of(own, core) + heads_of(other, 1 - core)
    return out.astype(jnp.bfloat16)


def solution(mesh):
    sizes = [n for _, n in SEG_SPLIT]
    devices = mesh.devices.reshape(
        *sizes, mesh.shape["frm"], mesh.shape["rec"]
    )
    fine = Mesh(devices, tuple(name for name, _ in SEG_SPLIT) + ("frm", "rec"))
    in_specs = (P("rec", SCAN_AXES, None), P(), P())
    out_specs = P("rec", SCAN_AXES, None)
    return jax.shard_map(shards, mesh=fine, in_specs=in_specs, out_specs=out_specs, check_vma=False)
```

```python
import jax
import jax.numpy as jnp
from jax import lax
from jax.sharding import Mesh, PartitionSpec as P

HEADS = 16
SPAN = 256

SEG_SPLIT = (("seg_z", 8), ("seg_y", 4), ("seg_x", 2))
SCAN_AXES = ("seg_z", "seg_y", "seg_x", "frm")


def features(t):
    return jnp.where(t > 0.0, t + 1.0, jnp.exp(jnp.minimum(t, 0.0)))


def tmap(f, *trees):
    return jax.tree.map(f, *trees)


def send(tree, axis, pairs):
    return tmap(lambda t: lax.ppermute(t, axis, perm=pairs), tree)


def swap(tree, axis):
    return send(tree, axis, [(0, 1), (1, 0)])


def forward(n, s):
    return [(i, i + s) for i in range(n - s)]


def part(tree, index, count):
    def one(t):
        size = t.shape[0] // count
        return lax.dynamic_slice_in_dim(t, index * size, size, axis=0)

    return tmap(one, tree)


def ordered(mine, other, first):
    lo = tmap(lambda a, b: jnp.where(first, a, b), mine, other)
    hi = tmap(lambda a, b: jnp.where(first, b, a), mine, other)
    return lo, hi


def keep(tree, cond):
    return tmap(lambda a: jnp.where(cond, a, jnp.zeros_like(a)), tree)


def joined(lo, hi):
    return tmap(lambda a, b: jnp.concatenate([a, b], axis=0), lo, hi)


def cyclic(n, s):
    return [(i, (i + s) % n) for i in range(n)]


def entering(total, carry):
    core = lax.axis_index("frm")
    xh = lax.axis_index("seg_x")
    y = lax.axis_index("seg_y")
    z = lax.axis_index("seg_z")
    n_y = lax.axis_size("seg_y")
    n_z = lax.axis_size("seg_z")
    add = lambda a, b: tmap(jnp.add, a, b)
    own_c = part(total, core, 2)
    got_c = swap(part(total, 1 - core, 2), "frm")
    lo, hi = ordered(own_c, got_c, core == 0)
    chip = add(lo, hi)
    came = [part(chip, y, n_y)] + [
        send(part(chip, (y + s) % n_y, n_y), "seg_y", cyclic(n_y, s)) for s in range(1, n_y)
    ]
    column = came[0]
    for c in came[1:]:
        column = add(column, c)
    before_z = tmap(jnp.zeros_like, column)
    left = right = column
    for r in range(1, n_z // 2 + 1):
        left = send(left, "seg_z", cyclic(n_z, 1))
        before_z = add(before_z, keep(left, z >= r))
        if r < n_z - r:
            right = send(right, "seg_z", cyclic(n_z, -1))
            before_z = add(before_z, keep(right, z + r >= n_z))
    before_z, carry = lax.optimization_barrier((before_z, carry))

    def for_row(t):
        out = before_z
        for s, c in enumerate(came):
            out = add(out, keep(c, (y - s) % n_y < t))
        return out

    pieces = [for_row(y)] + [
        send(for_row((y + s) % n_y), "seg_y", cyclic(n_y, s)) for s in range(1, n_y)
    ]
    order = (y - jnp.arange(n_y)) % n_y
    mine = tmap(
        lambda *p: jnp.stack(p)[order].reshape((-1,) + p[0].shape[1:]),
        *pieces,
    )
    half = add(mine, swap(add(mine, keep(chip, xh == 0)), "seg_x"))
    got = swap(add(half, keep(own_c, core == 0)), "frm")
    own = tmap(lambda a, c: jnp.where(core == 0, a, a + c), half, got_c)
    return (own, got), carry


def block_terms(phi_q, phi_k, values, span):
    rows, length, heads, dim = phi_q.shape
    count = length // span
    pq = phi_q.reshape(rows, count, span, heads, dim)
    pk = phi_k.reshape(rows, count, span, heads, dim)
    vv = values.reshape(rows, count, span, heads, dim)
    scores = jnp.einsum("rnihd,rnjhd->rnhij", pq, pk, preferred_element_type=jnp.float32)
    causal = jnp.arange(span)[:, None] >= jnp.arange(span)[None, :]
    scores = jnp.where(causal, scores, 0.0)
    den_local = jnp.sum(scores, axis=-1)
    weights = scores.astype(jnp.bfloat16)
    num_local = jnp.einsum("rnhij,rnjhd->rnihd", weights, vv, preferred_element_type=jnp.float32)
    kv_blocks = jnp.einsum("rnjhd,rnjhe->rnhde", pk, vv, preferred_element_type=jnp.float32)
    k_blocks = jnp.sum(pk, axis=2, dtype=jnp.float32)
    return (pq, num_local, den_local, kv_blocks, k_blocks)


def finish(pq, num_local, den_local, kv_blocks, k_blocks, prior_kv, prior_k):
    rows, count, span, heads, dim = pq.shape
    before_kv = jnp.cumsum(kv_blocks, axis=1) - kv_blocks + prior_kv[:, None]
    before_k = jnp.cumsum(k_blocks, axis=1) - k_blocks + prior_k[:, None]
    high = before_kv.astype(jnp.bfloat16)
    low = (before_kv - high.astype(jnp.float32)).astype(jnp.bfloat16)
    carried = jnp.einsum("rnihd,rnhde->rnihe", pq, high, preferred_element_type=jnp.float32)
    carried = carried + jnp.einsum("rnihd,rnhde->rnihe", pq, low, preferred_element_type=jnp.float32)
    num = num_local + carried
    pq32 = pq.astype(jnp.float32)
    den = jnp.transpose(den_local, (0, 1, 3, 2)) + jnp.sum(pq32 * before_k[:, :, None], axis=-1)
    result = (num / den[..., None]).astype(jnp.bfloat16)
    return result.reshape(rows, count * span, heads * dim)


def split_qkv(qkv):
    phi_q = features(qkv[:, :, 0].astype(jnp.float32)).astype(jnp.bfloat16)
    phi_k = features(qkv[:, :, 1].astype(jnp.float32)).astype(jnp.bfloat16)
    return (phi_q, phi_k, qkv[:, :, 2])


def shards(frames_in, w_qkv, w_out):
    rows, tok_local, width = frames_in.shape
    head_dim = width // HEADS
    def project(w, count):
        out = jnp.einsum("rtd,de->ret", frames_in, w, preferred_element_type=jnp.float32)
        out = out.astype(jnp.bfloat16).reshape(rows, count, HEADS, head_dim, tok_local)
        return jnp.transpose(out, (0, 4, 1, 2, 3))

    keys_values = project(w_qkv[:, width:], 2)
    queries = project(w_qkv[:, :width], 1)
    phi_q = features(queries[:, :, 0].astype(jnp.float32)).astype(jnp.bfloat16)
    phi_k = features(keys_values[:, :, 0].astype(jnp.float32)).astype(jnp.bfloat16)
    values = keys_values[:, :, 1]
    pq, num_local, den_local, kv_blocks, k_blocks = block_terms(phi_q, phi_k, values, SPAN)
    total_kv = jnp.sum(kv_blocks, axis=1)[0]
    total_k = jnp.sum(k_blocks, axis=1)[0]
    lanes = 128
    dense = total_kv.reshape(HEADS, -1, lanes)
    rows_kv = dense.shape[1]
    norm = jnp.pad(total_k, ((0, 0), (0, lanes - total_k.shape[1])))[:, None]
    (own, other), (num_local, den_local) = entering(
        jnp.concatenate([dense, norm], axis=1), (num_local, den_local)
    )
    core = lax.axis_index("frm")
    half_heads = HEADS // 2

    def heads_of(prior, which):
        first = which * half_heads
        pick = lambda t, axis: lax.dynamic_slice_in_dim(t, first, half_heads, axis=axis)
        prior_kv = prior[:, :rows_kv].reshape((half_heads,) + total_kv.shape[1:])
        prior_k = prior[:, rows_kv, : total_k.shape[1]]
        heads_out = finish(
            pick(pq, 3), pick(num_local, 3), pick(den_local, 2),
            pick(kv_blocks, 2), pick(k_blocks, 2), prior_kv[None], prior_k[None],
        )
        rows_w = lax.dynamic_slice_in_dim(w_out, first * head_dim, half_heads * head_dim, axis=0)
        return jnp.einsum("rtd,de->rte", heads_out, rows_w, preferred_element_type=jnp.float32)

    out = heads_of(own, core) + heads_of(other, 1 - core)
    return out.astype(jnp.bfloat16)


def solution(mesh):
    sizes = [n for _, n in SEG_SPLIT]
    devices = mesh.devices.reshape(
        *sizes, mesh.shape["frm"], mesh.shape["rec"]
    )
    fine = Mesh(devices, tuple(name for name, _ in SEG_SPLIT) + ("frm", "rec"))
    in_specs = (P("rec", SCAN_AXES, None), P(), P())
    out_specs = P("rec", SCAN_AXES, None)
    return jax.shard_map(shards, mesh=fine, in_specs=in_specs, out_specs=out_specs, check_vma=False)
```

```python
import jax
import jax.numpy as jnp
from jax import lax
from jax.sharding import Mesh, PartitionSpec as P

HEADS = 16
SPAN = 256

SEG_SPLIT = (("seg_z", 8), ("seg_y", 4), ("seg_x", 2))
SCAN_AXES = ("seg_z", "seg_y", "seg_x", "frm")


def features(t):
    return jnp.where(t > 0.0, t + 1.0, jnp.exp(jnp.minimum(t, 0.0)))


def tmap(f, *trees):
    return jax.tree.map(f, *trees)


def send(tree, axis, pairs):
    return tmap(lambda t: lax.ppermute(t, axis, perm=pairs), tree)


def swap(tree, axis):
    return send(tree, axis, [(0, 1), (1, 0)])


def forward(n, s):
    return [(i, i + s) for i in range(n - s)]


def part(tree, index, count):
    def one(t):
        size = t.shape[0] // count
        return lax.dynamic_slice_in_dim(t, index * size, size, axis=0)

    return tmap(one, tree)


def ordered(mine, other, first):
    lo = tmap(lambda a, b: jnp.where(first, a, b), mine, other)
    hi = tmap(lambda a, b: jnp.where(first, b, a), mine, other)
    return lo, hi


def keep(tree, cond):
    return tmap(lambda a: jnp.where(cond, a, jnp.zeros_like(a)), tree)


def joined(lo, hi):
    return tmap(lambda a, b: jnp.concatenate([a, b], axis=0), lo, hi)


def cyclic(n, s):
    return [(i, (i + s) % n) for i in range(n)]


def entering(total, carry):
    core = lax.axis_index("frm")
    xh = lax.axis_index("seg_x")
    y = lax.axis_index("seg_y")
    z = lax.axis_index("seg_z")
    n_y = lax.axis_size("seg_y")
    n_z = lax.axis_size("seg_z")
    add = lambda a, b: tmap(jnp.add, a, b)
    own_c = part(total, core, 2)
    got_c = swap(part(total, 1 - core, 2), "frm")
    lo, hi = ordered(own_c, got_c, core == 0)
    chip = add(lo, hi)
    came = [part(chip, y, n_y)] + [
        send(part(chip, (y + s) % n_y, n_y), "seg_y", cyclic(n_y, s)) for s in range(1, n_y)
    ]
    column = came[0]
    for c in came[1:]:
        column = add(column, c)
    before_z = tmap(jnp.zeros_like, column)
    left = right = column
    for r in range(1, n_z // 2 + 1):
        left = send(left, "seg_z", cyclic(n_z, 1))
        before_z = add(before_z, keep(left, z >= r))
        if r < n_z - r:
            right = send(right, "seg_z", cyclic(n_z, -1))
            before_z = add(before_z, keep(right, z + r >= n_z))
    before_z, carry = lax.optimization_barrier((before_z, carry))

    def for_row(t):
        out = before_z
        for s, c in enumerate(came):
            out = add(out, keep(c, (y - s) % n_y < t))
        return out

    pieces = [for_row(y)] + [
        send(for_row((y + s) % n_y), "seg_y", cyclic(n_y, s)) for s in range(1, n_y)
    ]
    order = (y - jnp.arange(n_y)) % n_y
    mine = tmap(
        lambda *p: jnp.stack(p)[order].reshape((-1,) + p[0].shape[1:]),
        *pieces,
    )
    half = add(mine, swap(add(mine, keep(chip, xh == 0)), "seg_x"))
    got = swap(add(half, keep(own_c, core == 0)), "frm")
    own = tmap(lambda a, c: jnp.where(core == 0, a, a + c), half, got_c)
    return (own, got), carry


def block_terms(phi_q, phi_k, values, span):
    rows, length, heads, dim = phi_q.shape
    count = length // span
    pq = phi_q.reshape(rows, count, span, heads, dim)
    pk = phi_k.reshape(rows, count, span, heads, dim)
    vv = values.reshape(rows, count, span, heads, dim)
    scores = jnp.einsum("rnihd,rnjhd->rnhij", pq, pk, preferred_element_type=jnp.float32)
    causal = jnp.arange(span)[:, None] >= jnp.arange(span)[None, :]
    scores = jnp.where(causal, scores, 0.0)
    den_local = jnp.sum(scores, axis=-1)
    weights = scores.astype(jnp.bfloat16)
    num_local = jnp.einsum("rnhij,rnjhd->rnihd", weights, vv, preferred_element_type=jnp.float32)
    kv_blocks = jnp.einsum("rnjhd,rnjhe->rnhde", pk, vv, preferred_element_type=jnp.float32)
    k_blocks = jnp.sum(pk, axis=2, dtype=jnp.float32)
    return (pq, num_local, den_local, kv_blocks, k_blocks)


def finish(pq, num_local, den_local, kv_blocks, k_blocks, prior_kv, prior_k):
    rows, count, span, heads, dim = pq.shape
    before_kv = jnp.cumsum(kv_blocks, axis=1) - kv_blocks + prior_kv[:, None]
    before_k = jnp.cumsum(k_blocks, axis=1) - k_blocks + prior_k[:, None]
    pq32 = pq.astype(jnp.float32)
    num = num_local + jnp.einsum(
        "rnihd,rnhde->rnihe", pq32, before_kv, precision=lax.Precision.HIGHEST
    )
    den = jnp.transpose(den_local, (0, 1, 3, 2)) + jnp.sum(pq32 * before_k[:, :, None], axis=-1)
    result = (num / den[..., None]).astype(jnp.bfloat16)
    return result.reshape(rows, count * span, heads * dim)


def split_qkv(qkv):
    phi_q = features(qkv[:, :, 0].astype(jnp.float32)).astype(jnp.bfloat16)
    phi_k = features(qkv[:, :, 1].astype(jnp.float32)).astype(jnp.bfloat16)
    return (phi_q, phi_k, qkv[:, :, 2])


def shards(frames_in, w_qkv, w_out):
    rows, tok_local, width = frames_in.shape
    head_dim = width // HEADS
    def project(w, count):
        out = jnp.einsum("rtd,de->ret", frames_in, w, preferred_element_type=jnp.float32)
        out = out.astype(jnp.bfloat16).reshape(rows, count, HEADS, head_dim, tok_local)
        return jnp.transpose(out, (0, 4, 1, 2, 3))

    keys_values = project(w_qkv[:, width:], 2)
    queries = project(w_qkv[:, :width], 1)
    phi_q = features(queries[:, :, 0].astype(jnp.float32)).astype(jnp.bfloat16)
    phi_k = features(keys_values[:, :, 0].astype(jnp.float32)).astype(jnp.bfloat16)
    values = keys_values[:, :, 1]
    pq, num_local, den_local, kv_blocks, k_blocks = block_terms(phi_q, phi_k, values, SPAN)
    total_kv = jnp.sum(kv_blocks, axis=1)[0]
    total_k = jnp.sum(k_blocks, axis=1)[0]
    lanes = 128
    dense = total_kv.reshape(HEADS, -1, lanes)
    rows_kv = dense.shape[1]
    norm = jnp.pad(total_k, ((0, 0), (0, lanes - total_k.shape[1])))[:, None]
    (own, other), (num_local, den_local) = entering(
        jnp.concatenate([dense, norm], axis=1), (num_local, den_local)
    )
    core = lax.axis_index("frm")
    half_heads = HEADS // 2

    def heads_of(prior, which):
        first = which * half_heads
        pick = lambda t, axis: lax.dynamic_slice_in_dim(t, first, half_heads, axis=axis)
        prior_kv = prior[:, :rows_kv].reshape((half_heads,) + total_kv.shape[1:])
        prior_k = prior[:, rows_kv, : total_k.shape[1]]
        heads_out = finish(
            pick(pq, 3), pick(num_local, 3), pick(den_local, 2),
            pick(kv_blocks, 2), pick(k_blocks, 2), prior_kv[None], prior_k[None],
        )
        rows_w = lax.dynamic_slice_in_dim(w_out, first * head_dim, half_heads * head_dim, axis=0)
        return jnp.einsum("rtd,de->rte", heads_out, rows_w, preferred_element_type=jnp.float32)

    out = heads_of(own, core) + heads_of(other, 1 - core)
    return out.astype(jnp.bfloat16)


def solution(mesh):
    sizes = [n for _, n in SEG_SPLIT]
    devices = mesh.devices.reshape(
        *sizes, mesh.shape["frm"], mesh.shape["rec"]
    )
    fine = Mesh(devices, tuple(name for name, _ in SEG_SPLIT) + ("frm", "rec"))
    in_specs = (P("rec", SCAN_AXES, None), P(), P())
    out_specs = P("rec", SCAN_AXES, None)
    return jax.shard_map(shards, mesh=fine, in_specs=in_specs, out_specs=out_specs, check_vma=False)
```

```python
import jax
import jax.numpy as jnp
from jax import lax
from jax.sharding import Mesh, PartitionSpec as P

HEADS = 16
SPAN = 256

SEG_SPLIT = (("seg_z", 8), ("seg_y", 4), ("seg_x", 2))
SCAN_AXES = ("seg_z", "seg_y", "seg_x", "frm")


def features(t):
    return jnp.where(t > 0.0, t + 1.0, jnp.exp(jnp.minimum(t, 0.0)))


def tmap(f, *trees):
    return jax.tree.map(f, *trees)


def send(tree, axis, pairs):
    return tmap(lambda t: lax.ppermute(t, axis, perm=pairs), tree)


def swap(tree, axis):
    return send(tree, axis, [(0, 1), (1, 0)])


def forward(n, s):
    return [(i, i + s) for i in range(n - s)]


def part(tree, index, count):
    def one(t):
        size = t.shape[0] // count
        return lax.dynamic_slice_in_dim(t, index * size, size, axis=0)

    return tmap(one, tree)


def ordered(mine, other, first):
    lo = tmap(lambda a, b: jnp.where(first, a, b), mine, other)
    hi = tmap(lambda a, b: jnp.where(first, b, a), mine, other)
    return lo, hi


def keep(tree, cond):
    return tmap(lambda a: jnp.where(cond, a, jnp.zeros_like(a)), tree)


def joined(lo, hi):
    return tmap(lambda a, b: jnp.concatenate([a, b], axis=0), lo, hi)


def cyclic(n, s):
    return [(i, (i + s) % n) for i in range(n)]


def entering(total, carry):
    core = lax.axis_index("frm")
    xh = lax.axis_index("seg_x")
    y = lax.axis_index("seg_y")
    z = lax.axis_index("seg_z")
    n_y = lax.axis_size("seg_y")
    n_z = lax.axis_size("seg_z")
    add = lambda a, b: tmap(jnp.add, a, b)
    own_c = part(total, core, 2)
    got_c = swap(part(total, 1 - core, 2), "frm")
    lo, hi = ordered(own_c, got_c, core == 0)
    chip = add(lo, hi)
    came = [part(chip, y, n_y)] + [
        send(part(chip, (y + s) % n_y, n_y), "seg_y", cyclic(n_y, s)) for s in range(1, n_y)
    ]
    column = came[0]
    for c in came[1:]:
        column = add(column, c)
    before_z = tmap(jnp.zeros_like, column)
    left = right = column
    for r in range(1, n_z // 2 + 1):
        left = send(left, "seg_z", cyclic(n_z, 1))
        before_z = add(before_z, keep(left, z >= r))
        if r < n_z - r:
            right = send(right, "seg_z", cyclic(n_z, -1))
            before_z = add(before_z, keep(right, z + r >= n_z))
    before_z, carry = lax.optimization_barrier((before_z, carry))

    def for_row(t):
        out = before_z
        for s, c in enumerate(came):
            out = add(out, keep(c, (y - s) % n_y < t))
        return out

    pieces = [for_row(y)] + [
        send(for_row((y + s) % n_y), "seg_y", cyclic(n_y, s)) for s in range(1, n_y)
    ]
    order = (y - jnp.arange(n_y)) % n_y
    mine = tmap(
        lambda *p: jnp.stack(p)[order].reshape((-1,) + p[0].shape[1:]),
        *pieces,
    )
    half = add(mine, swap(add(mine, keep(chip, xh == 0)), "seg_x"))
    got = swap(add(half, keep(own_c, core == 0)), "frm")
    own = tmap(lambda a, c: jnp.where(core == 0, a, a + c), half, got_c)
    return (own, got), carry


def block_terms(phi_q, phi_k, values, span):
    rows, length, heads, dim = phi_q.shape
    count = length // span
    pq = phi_q.reshape(rows, count, span, heads, dim)
    pk = phi_k.reshape(rows, count, span, heads, dim)
    vv = values.reshape(rows, count, span, heads, dim)
    scores = jnp.einsum("rnihd,rnjhd->rnhij", pq, pk, preferred_element_type=jnp.float32)
    causal = jnp.arange(span)[:, None] >= jnp.arange(span)[None, :]
    scores = jnp.where(causal, scores, 0.0)
    den_local = jnp.sum(scores, axis=-1)
    weights = scores.astype(jnp.bfloat16)
    num_local = jnp.einsum("rnhij,rnjhd->rnihd", weights, vv, preferred_element_type=jnp.float32)
    kv_blocks = jnp.einsum("rnjhd,rnjhe->rnhde", pk, vv, preferred_element_type=jnp.float32)
    k_blocks = jnp.sum(pk, axis=2, dtype=jnp.float32)
    return (pq, num_local, den_local, kv_blocks, k_blocks)


def finish(pq, num_local, den_local, kv_blocks, k_blocks, prior_kv, prior_k):
    rows, count, span, heads, dim = pq.shape
    before_kv = jnp.cumsum(kv_blocks, axis=1) - kv_blocks + prior_kv[:, None]
    before_k = jnp.cumsum(k_blocks, axis=1) - k_blocks + prior_k[:, None]
    pq32 = pq.astype(jnp.float32)
    num = num_local + jnp.einsum(
        "rnihd,rnhde->rnihe", pq32, before_kv, precision=lax.Precision.HIGHEST
    )
    den = jnp.transpose(den_local, (0, 1, 3, 2)) + jnp.sum(pq32 * before_k[:, :, None], axis=-1)
    result = (num / den[..., None]).astype(jnp.bfloat16)
    return result.reshape(rows, count * span, heads * dim)


def split_qkv(qkv):
    phi_q = features(qkv[:, :, 0].astype(jnp.float32)).astype(jnp.bfloat16)
    phi_k = features(qkv[:, :, 1].astype(jnp.float32)).astype(jnp.bfloat16)
    return (phi_q, phi_k, qkv[:, :, 2])


def shards(frames_in, w_qkv, w_out):
    rows, tok_local, width = frames_in.shape
    head_dim = width // HEADS
    def project(w, count):
        out = jnp.einsum("rtd,de->ret", frames_in, w, preferred_element_type=jnp.float32)
        out = out.astype(jnp.bfloat16).reshape(rows, count, HEADS, head_dim, tok_local)
        return jnp.transpose(out, (0, 4, 1, 2, 3))

    keys_values = project(w_qkv[:, width:], 2)
    queries = project(w_qkv[:, :width], 1)
    phi_q = features(queries[:, :, 0].astype(jnp.float32)).astype(jnp.bfloat16)
    phi_k = features(keys_values[:, :, 0].astype(jnp.float32)).astype(jnp.bfloat16)
    values = keys_values[:, :, 1]
    pq, num_local, den_local, kv_blocks, k_blocks = block_terms(phi_q, phi_k, values, SPAN)
    total_kv = jnp.sum(kv_blocks, axis=1)[0]
    total_k = jnp.sum(k_blocks, axis=1)[0]
    lanes = 128
    dense = total_kv.reshape(HEADS, -1, lanes)
    rows_kv = dense.shape[1]
    norm = jnp.pad(total_k, ((0, 0), (0, lanes - total_k.shape[1])))[:, None]
    (own, other), (num_local, den_local) = entering(
        jnp.concatenate([dense, norm], axis=1), (num_local, den_local)
    )
    core = lax.axis_index("frm")
    half_heads = HEADS // 2

    def heads_of(prior, which):
        first = which * half_heads
        pick = lambda t, axis: lax.dynamic_slice_in_dim(t, first, half_heads, axis=axis)
        prior_kv = prior[:, :rows_kv].reshape((half_heads,) + total_kv.shape[1:])
        prior_k = prior[:, rows_kv, : total_k.shape[1]]
        heads_out = finish(
            pick(pq, 3), pick(num_local, 3), pick(den_local, 2),
            pick(kv_blocks, 2), pick(k_blocks, 2), prior_kv[None], prior_k[None],
        )
        rows_w = lax.dynamic_slice_in_dim(w_out, first * head_dim, half_heads * head_dim, axis=0)
        return jnp.einsum("rtd,de->rte", heads_out, rows_w, preferred_element_type=jnp.float32)

    mine = heads_of(own, core)
    other, mine = lax.optimization_barrier((other, mine))
    out = mine + heads_of(other, 1 - core)
    return out.astype(jnp.bfloat16)


def solution(mesh):
    sizes = [n for _, n in SEG_SPLIT]
    devices = mesh.devices.reshape(
        *sizes, mesh.shape["frm"], mesh.shape["rec"]
    )
    fine = Mesh(devices, tuple(name for name, _ in SEG_SPLIT) + ("frm", "rec"))
    in_specs = (P("rec", SCAN_AXES, None), P(), P())
    out_specs = P("rec", SCAN_AXES, None)
    return jax.shard_map(shards, mesh=fine, in_specs=in_specs, out_specs=out_specs, check_vma=False)
```

```python
import jax
import jax.numpy as jnp
from jax import lax
from jax.sharding import Mesh, PartitionSpec as P

HEADS = 16
SPAN = 256

SEG_SPLIT = (("seg_z", 8), ("seg_y", 4), ("seg_x", 2))
SCAN_AXES = ("seg_z", "seg_y", "seg_x", "frm")


def features(t):
    return jnp.where(t > 0.0, t + 1.0, jnp.exp(jnp.minimum(t, 0.0)))


def tmap(f, *trees):
    return jax.tree.map(f, *trees)


def send(tree, axis, pairs):
    return tmap(lambda t: lax.ppermute(t, axis, perm=pairs), tree)


def swap(tree, axis):
    return send(tree, axis, [(0, 1), (1, 0)])


def forward(n, s):
    return [(i, i + s) for i in range(n - s)]


def part(tree, index, count):
    def one(t):
        size = t.shape[0] // count
        return lax.dynamic_slice_in_dim(t, index * size, size, axis=0)

    return tmap(one, tree)


def ordered(mine, other, first):
    lo = tmap(lambda a, b: jnp.where(first, a, b), mine, other)
    hi = tmap(lambda a, b: jnp.where(first, b, a), mine, other)
    return lo, hi


def keep(tree, cond):
    return tmap(lambda a: jnp.where(cond, a, jnp.zeros_like(a)), tree)


def joined(lo, hi):
    return tmap(lambda a, b: jnp.concatenate([a, b], axis=0), lo, hi)


def cyclic(n, s):
    return [(i, (i + s) % n) for i in range(n)]


def entering(total, carry):
    core = lax.axis_index("frm")
    xh = lax.axis_index("seg_x")
    y = lax.axis_index("seg_y")
    z = lax.axis_index("seg_z")
    n_y = lax.axis_size("seg_y")
    n_z = lax.axis_size("seg_z")
    add = lambda a, b: tmap(jnp.add, a, b)
    own_c = part(total, core, 2)
    got_c = swap(part(total, 1 - core, 2), "frm")
    lo, hi = ordered(own_c, got_c, core == 0)
    chip = add(lo, hi)
    came = [part(chip, y, n_y)] + [
        send(part(chip, (y + s) % n_y, n_y), "seg_y", cyclic(n_y, s)) for s in range(1, n_y)
    ]
    column = came[0]
    for c in came[1:]:
        column = add(column, c)
    column = add(column, swap(column, "seg_x"))
    stacked = jnp.stack(came)
    column, stacked = lax.optimization_barrier((column, stacked))
    theirs = swap(jnp.concatenate([stacked.reshape((-1,) + chip.shape[1:]), chip], axis=0), "seg_x")
    their_came = theirs[: stacked.shape[0] * stacked.shape[1]].reshape(stacked.shape)
    their_chip = theirs[stacked.shape[0] * stacked.shape[1]:]
    before_z = tmap(jnp.zeros_like, column)
    left = right = column
    for r in range(1, n_z // 2 + 1):
        left = send(left, "seg_z", cyclic(n_z, 1))
        before_z = add(before_z, keep(left, z >= r))
        if r < n_z - r:
            right = send(right, "seg_z", cyclic(n_z, -1))
            before_z = add(before_z, keep(right, z + r >= n_z))
    before_z, carry = lax.optimization_barrier((before_z, carry))

    def for_row(t):
        out = before_z
        for s, c in enumerate(came):
            out = add(out, keep(c + their_came[s], (y - s) % n_y < t))
        return out

    pieces = [for_row(y)] + [
        send(for_row((y + s) % n_y), "seg_y", cyclic(n_y, s)) for s in range(1, n_y)
    ]
    order = (y - jnp.arange(n_y)) % n_y
    mine = tmap(
        lambda *p: jnp.stack(p)[order].reshape((-1,) + p[0].shape[1:]),
        *pieces,
    )
    half = add(mine, keep(their_chip, xh == 1))
    got = swap(add(half, keep(own_c, core == 0)), "frm")
    own = tmap(lambda a, c: jnp.where(core == 0, a, a + c), half, got_c)
    return (own, got), carry


def block_terms(phi_q, phi_k, values, span):
    rows, length, heads, dim = phi_q.shape
    count = length // span
    pq = phi_q.reshape(rows, count, span, heads, dim)
    pk = phi_k.reshape(rows, count, span, heads, dim)
    vv = values.reshape(rows, count, span, heads, dim)
    scores = jnp.einsum("rnihd,rnjhd->rnhij", pq, pk, preferred_element_type=jnp.float32)
    causal = jnp.arange(span)[:, None] >= jnp.arange(span)[None, :]
    scores = jnp.where(causal, scores, 0.0)
    den_local = jnp.sum(scores, axis=-1)
    weights = scores.astype(jnp.bfloat16)
    num_local = jnp.einsum("rnhij,rnjhd->rnihd", weights, vv, preferred_element_type=jnp.float32)
    kv_blocks = jnp.einsum("rnjhd,rnjhe->rnhde", pk, vv, preferred_element_type=jnp.float32)
    k_blocks = jnp.sum(pk, axis=2, dtype=jnp.float32)
    return (pq, num_local, den_local, kv_blocks, k_blocks)


def finish(pq, num_local, den_local, kv_blocks, k_blocks, prior_kv, prior_k):
    rows, count, span, heads, dim = pq.shape
    before_kv = jnp.cumsum(kv_blocks, axis=1) - kv_blocks + prior_kv[:, None]
    before_k = jnp.cumsum(k_blocks, axis=1) - k_blocks + prior_k[:, None]
    pq32 = pq.astype(jnp.float32)
    num = num_local + jnp.einsum(
        "rnihd,rnhde->rnihe", pq32, before_kv, precision=lax.Precision.HIGHEST
    )
    den = jnp.transpose(den_local, (0, 1, 3, 2)) + jnp.sum(pq32 * before_k[:, :, None], axis=-1)
    result = (num / den[..., None]).astype(jnp.bfloat16)
    return result.reshape(rows, count * span, heads * dim)


def split_qkv(qkv):
    phi_q = features(qkv[:, :, 0].astype(jnp.float32)).astype(jnp.bfloat16)
    phi_k = features(qkv[:, :, 1].astype(jnp.float32)).astype(jnp.bfloat16)
    return (phi_q, phi_k, qkv[:, :, 2])


def shards(frames_in, w_qkv, w_out):
    rows, tok_local, width = frames_in.shape
    head_dim = width // HEADS
    def project(w, count):
        out = jnp.einsum("rtd,de->ret", frames_in, w, preferred_element_type=jnp.float32)
        out = out.astype(jnp.bfloat16).reshape(rows, count, HEADS, head_dim, tok_local)
        return jnp.transpose(out, (0, 4, 1, 2, 3))

    keys_values = project(w_qkv[:, width:], 2)
    queries = project(w_qkv[:, :width], 1)
    phi_q = features(queries[:, :, 0].astype(jnp.float32)).astype(jnp.bfloat16)
    phi_k = features(keys_values[:, :, 0].astype(jnp.float32)).astype(jnp.bfloat16)
    values = keys_values[:, :, 1]
    pq, num_local, den_local, kv_blocks, k_blocks = block_terms(phi_q, phi_k, values, SPAN)
    total_kv = jnp.sum(kv_blocks, axis=1)[0]
    total_k = jnp.sum(k_blocks, axis=1)[0]
    lanes = 128
    dense = total_kv.reshape(HEADS, -1, lanes)
    rows_kv = dense.shape[1]
    norm = jnp.pad(total_k, ((0, 0), (0, lanes - total_k.shape[1])))[:, None]
    (own, other), (num_local, den_local) = entering(
        jnp.concatenate([dense, norm], axis=1), (num_local, den_local)
    )
    core = lax.axis_index("frm")
    half_heads = HEADS // 2

    def heads_of(prior, which):
        first = which * half_heads
        pick = lambda t, axis: lax.dynamic_slice_in_dim(t, first, half_heads, axis=axis)
        prior_kv = prior[:, :rows_kv].reshape((half_heads,) + total_kv.shape[1:])
        prior_k = prior[:, rows_kv, : total_k.shape[1]]
        heads_out = finish(
            pick(pq, 3), pick(num_local, 3), pick(den_local, 2),
            pick(kv_blocks, 2), pick(k_blocks, 2), prior_kv[None], prior_k[None],
        )
        rows_w = lax.dynamic_slice_in_dim(w_out, first * head_dim, half_heads * head_dim, axis=0)
        return jnp.einsum("rtd,de->rte", heads_out, rows_w, preferred_element_type=jnp.float32)

    out = heads_of(own, core) + heads_of(other, 1 - core)
    return out.astype(jnp.bfloat16)


def solution(mesh):
    sizes = [n for _, n in SEG_SPLIT]
    devices = mesh.devices.reshape(
        *sizes, mesh.shape["frm"], mesh.shape["rec"]
    )
    fine = Mesh(devices, tuple(name for name, _ in SEG_SPLIT) + ("frm", "rec"))
    in_specs = (P("rec", SCAN_AXES, None), P(), P())
    out_specs = P("rec", SCAN_AXES, None)
    return jax.shard_map(shards, mesh=fine, in_specs=in_specs, out_specs=out_specs, check_vma=False)
```

```python
import jax
import jax.numpy as jnp
from jax import lax
from jax.sharding import Mesh, PartitionSpec as P

HEADS = 16
SPAN = 256

SEG_SPLIT = (("seg_z", 8), ("seg_y", 4), ("seg_x", 2))
SCAN_AXES = ("seg_z", "seg_y", "seg_x", "frm")


def features(t):
    return jnp.where(t > 0.0, t + 1.0, jnp.exp(jnp.minimum(t, 0.0)))


def tmap(f, *trees):
    return jax.tree.map(f, *trees)


def send(tree, axis, pairs):
    return tmap(lambda t: lax.ppermute(t, axis, perm=pairs), tree)


def swap(tree, axis):
    return send(tree, axis, [(0, 1), (1, 0)])


def forward(n, s):
    return [(i, i + s) for i in range(n - s)]


def part(tree, index, count):
    def one(t):
        size = t.shape[0] // count
        return lax.dynamic_slice_in_dim(t, index * size, size, axis=0)

    return tmap(one, tree)


def ordered(mine, other, first):
    lo = tmap(lambda a, b: jnp.where(first, a, b), mine, other)
    hi = tmap(lambda a, b: jnp.where(first, b, a), mine, other)
    return lo, hi


def keep(tree, cond):
    return tmap(lambda a: jnp.where(cond, a, jnp.zeros_like(a)), tree)


def joined(lo, hi):
    return tmap(lambda a, b: jnp.concatenate([a, b], axis=0), lo, hi)


def cyclic(n, s):
    return [(i, (i + s) % n) for i in range(n)]


def entering(total, carry):
    core = lax.axis_index("frm")
    xh = lax.axis_index("seg_x")
    y = lax.axis_index("seg_y")
    z = lax.axis_index("seg_z")
    n_y = lax.axis_size("seg_y")
    n_z = lax.axis_size("seg_z")
    add = lambda a, b: tmap(jnp.add, a, b)
    first, second = jnp.split(total, 2, axis=0)
    own_c = jnp.where(core == 0, first, second)
    got_c = swap(jnp.where(core == 0, second, first), "frm")
    lo, hi = ordered(own_c, got_c, core == 0)
    chip = add(lo, hi)
    came = [part(chip, y, n_y)] + [
        send(part(chip, (y + s) % n_y, n_y), "seg_y", cyclic(n_y, s)) for s in range(1, n_y)
    ]
    column = came[0]
    for c in came[1:]:
        column = add(column, c)
    before_z = tmap(jnp.zeros_like, column)
    left = right = column
    for r in range(1, n_z // 2 + 1):
        left = send(left, "seg_z", cyclic(n_z, 1))
        before_z = add(before_z, keep(left, z >= r))
        if r < n_z - r:
            right = send(right, "seg_z", cyclic(n_z, -1))
            before_z = add(before_z, keep(right, z + r >= n_z))
    before_z, carry = lax.optimization_barrier((before_z, carry))

    def for_row(t):
        out = before_z
        for s, c in enumerate(came):
            out = add(out, keep(c, (y - s) % n_y < t))
        return out

    pieces = [for_row(y)] + [
        send(for_row((y + s) % n_y), "seg_y", cyclic(n_y, s)) for s in range(1, n_y)
    ]
    order = (y - jnp.arange(n_y)) % n_y
    mine = tmap(
        lambda *p: jnp.stack(p)[order].reshape((-1,) + p[0].shape[1:]),
        *pieces,
    )
    half = add(mine, swap(add(mine, keep(chip, xh == 0)), "seg_x"))
    got = swap(add(half, keep(own_c, core == 0)), "frm")
    own = tmap(lambda a, c: jnp.where(core == 0, a, a + c), half, got_c)
    return (own, got), carry


def block_terms(phi_q, phi_k, values, span):
    rows, length, heads, dim = phi_q.shape
    count = length // span
    pq = phi_q.reshape(rows, count, span, heads, dim)
    pk = phi_k.reshape(rows, count, span, heads, dim)
    vv = values.reshape(rows, count, span, heads, dim)
    scores = jnp.einsum("rnihd,rnjhd->rnhij", pq, pk, preferred_element_type=jnp.float32)
    causal = jnp.arange(span)[:, None] >= jnp.arange(span)[None, :]
    scores = jnp.where(causal, scores, 0.0)
    den_local = jnp.sum(scores, axis=-1)
    weights = scores.astype(jnp.bfloat16)
    num_local = jnp.einsum("rnhij,rnjhd->rnihd", weights, vv, preferred_element_type=jnp.float32)
    kv_blocks = jnp.einsum("rnjhd,rnjhe->rnhde", pk, vv, preferred_element_type=jnp.float32)
    k_blocks = jnp.sum(pk, axis=2, dtype=jnp.float32)
    return (pq, num_local, den_local, kv_blocks, k_blocks)


def finish(pq, num_local, den_local, kv_blocks, k_blocks, prior_kv, prior_k):
    rows, count, span, heads, dim = pq.shape
    before_kv = jnp.cumsum(kv_blocks, axis=1) - kv_blocks + prior_kv[:, None]
    before_k = jnp.cumsum(k_blocks, axis=1) - k_blocks + prior_k[:, None]
    pq32 = pq.astype(jnp.float32)
    num = num_local + jnp.einsum(
        "rnihd,rnhde->rnihe", pq32, before_kv, precision=lax.Precision.HIGHEST
    )
    den = jnp.transpose(den_local, (0, 1, 3, 2)) + jnp.sum(pq32 * before_k[:, :, None], axis=-1)
    result = (num / den[..., None]).astype(jnp.bfloat16)
    return result.reshape(rows, count * span, heads * dim)


def split_qkv(qkv):
    phi_q = features(qkv[:, :, 0].astype(jnp.float32)).astype(jnp.bfloat16)
    phi_k = features(qkv[:, :, 1].astype(jnp.float32)).astype(jnp.bfloat16)
    return (phi_q, phi_k, qkv[:, :, 2])


def shards(frames_in, w_qkv, w_out):
    rows, tok_local, width = frames_in.shape
    head_dim = width // HEADS
    def project(w, count):
        out = jnp.einsum("rtd,de->ret", frames_in, w, preferred_element_type=jnp.float32)
        out = out.astype(jnp.bfloat16).reshape(rows, count, HEADS, head_dim, tok_local)
        return jnp.transpose(out, (0, 4, 1, 2, 3))

    keys_values = project(w_qkv[:, width:], 2)
    queries = project(w_qkv[:, :width], 1)
    phi_q = features(queries[:, :, 0].astype(jnp.float32)).astype(jnp.bfloat16)
    phi_k = features(keys_values[:, :, 0].astype(jnp.float32)).astype(jnp.bfloat16)
    values = keys_values[:, :, 1]
    pq, num_local, den_local, kv_blocks, k_blocks = block_terms(phi_q, phi_k, values, SPAN)
    total_kv = jnp.sum(kv_blocks, axis=1)[0]
    total_k = jnp.sum(k_blocks, axis=1)[0]
    lanes = 128
    dense = total_kv.reshape(HEADS, -1, lanes)
    rows_kv = dense.shape[1]
    norm = jnp.pad(total_k, ((0, 0), (0, lanes - total_k.shape[1])))[:, None]
    (own, other), (num_local, den_local) = entering(
        jnp.concatenate([dense, norm], axis=1), (num_local, den_local)
    )
    core = lax.axis_index("frm")
    half_heads = HEADS // 2

    def heads_of(prior, which):
        first = which * half_heads
        pick = lambda t, axis: lax.dynamic_slice_in_dim(t, first, half_heads, axis=axis)
        prior_kv = prior[:, :rows_kv].reshape((half_heads,) + total_kv.shape[1:])
        prior_k = prior[:, rows_kv, : total_k.shape[1]]
        heads_out = finish(
            pick(pq, 3), pick(num_local, 3), pick(den_local, 2),
            pick(kv_blocks, 2), pick(k_blocks, 2), prior_kv[None], prior_k[None],
        )
        rows_w = lax.dynamic_slice_in_dim(w_out, first * head_dim, half_heads * head_dim, axis=0)
        return jnp.einsum("rtd,de->rte", heads_out, rows_w, preferred_element_type=jnp.float32)

    out = heads_of(own, core) + heads_of(other, 1 - core)
    return out.astype(jnp.bfloat16)


def solution(mesh):
    sizes = [n for _, n in SEG_SPLIT]
    devices = mesh.devices.reshape(
        *sizes, mesh.shape["frm"], mesh.shape["rec"]
    )
    fine = Mesh(devices, tuple(name for name, _ in SEG_SPLIT) + ("frm", "rec"))
    in_specs = (P("rec", SCAN_AXES, None), P(), P())
    out_specs = P("rec", SCAN_AXES, None)
    return jax.shard_map(shards, mesh=fine, in_specs=in_specs, out_specs=out_specs, check_vma=False)
```

```python
import jax
import jax.numpy as jnp
from jax import lax
from jax.sharding import Mesh, PartitionSpec as P

HEADS = 16
SPAN = 256

SEG_SPLIT = (("seg_z", 8), ("seg_y", 4), ("seg_x", 2))
SCAN_AXES = ("seg_z", "seg_y", "seg_x", "frm")


def features(t):
    return jnp.where(t > 0.0, t + 1.0, jnp.exp(jnp.minimum(t, 0.0)))


def tmap(f, *trees):
    return jax.tree.map(f, *trees)


def send(tree, axis, pairs):
    return tmap(lambda t: lax.ppermute(t, axis, perm=pairs), tree)


def swap(tree, axis):
    return send(tree, axis, [(0, 1), (1, 0)])


def forward(n, s):
    return [(i, i + s) for i in range(n - s)]


def part(tree, index, count):
    def one(t):
        size = t.shape[0] // count
        return lax.dynamic_slice_in_dim(t, index * size, size, axis=0)

    return tmap(one, tree)


def ordered(mine, other, first):
    lo = tmap(lambda a, b: jnp.where(first, a, b), mine, other)
    hi = tmap(lambda a, b: jnp.where(first, b, a), mine, other)
    return lo, hi


def keep(tree, cond):
    return tmap(lambda a: jnp.where(cond, a, jnp.zeros_like(a)), tree)


def joined(lo, hi):
    return tmap(lambda a, b: jnp.concatenate([a, b], axis=0), lo, hi)


def cyclic(n, s):
    return [(i, (i + s) % n) for i in range(n)]


def entering(total, carry):
    core = lax.axis_index("frm")
    xh = lax.axis_index("seg_x")
    y = lax.axis_index("seg_y")
    z = lax.axis_index("seg_z")
    n_y = lax.axis_size("seg_y")
    n_z = lax.axis_size("seg_z")
    add = lambda a, b: tmap(jnp.add, a, b)
    own_c = part(total, core, 2)
    got_c = swap(part(total, 1 - core, 2), "frm")
    lo, hi = ordered(own_c, got_c, core == 0)
    chip = add(lo, hi)
    came = [part(chip, y, n_y)] + [
        send(part(chip, (y + s) % n_y, n_y), "seg_y", cyclic(n_y, s)) for s in range(1, n_y)
    ]
    column = came[0]
    for c in came[1:]:
        column = add(column, c)
    planes = lax.all_gather(column, "seg_z", axis=0)
    earlier = lax.broadcasted_iota(jnp.int32, planes.shape, 0) < z
    before_z = jnp.sum(jnp.where(earlier, planes, 0.0), axis=0)

    def for_row(t):
        out = before_z
        for s, c in enumerate(came):
            out = add(out, keep(c, (y - s) % n_y < t))
        return out

    pieces = [for_row(y)] + [
        send(for_row((y + s) % n_y), "seg_y", cyclic(n_y, s)) for s in range(1, n_y)
    ]
    order = (y - jnp.arange(n_y)) % n_y
    mine = tmap(
        lambda *p: jnp.stack(p)[order].reshape((-1,) + p[0].shape[1:]),
        *pieces,
    )
    mine, carry = lax.optimization_barrier((mine, carry))
    half = add(mine, swap(add(mine, keep(chip, xh == 0)), "seg_x"))
    got = swap(add(half, keep(own_c, core == 0)), "frm")
    own = tmap(lambda a, c: jnp.where(core == 0, a, a + c), half, got_c)
    return (own, got), carry


def block_terms(phi_q, phi_k, values, span):
    rows, length, heads, dim = phi_q.shape
    count = length // span
    pq = phi_q.reshape(rows, count, span, heads, dim)
    pk = phi_k.reshape(rows, count, span, heads, dim)
    vv = values.reshape(rows, count, span, heads, dim)
    scores = jnp.einsum("rnihd,rnjhd->rnhij", pq, pk, preferred_element_type=jnp.float32)
    causal = jnp.arange(span)[:, None] >= jnp.arange(span)[None, :]
    scores = jnp.where(causal, scores, 0.0)
    den_local = jnp.sum(scores, axis=-1)
    weights = scores.astype(jnp.bfloat16)
    num_local = jnp.einsum("rnhij,rnjhd->rnihd", weights, vv, preferred_element_type=jnp.float32)
    kv_blocks = jnp.einsum("rnjhd,rnjhe->rnhde", pk, vv, preferred_element_type=jnp.float32)
    k_blocks = jnp.sum(pk, axis=2, dtype=jnp.float32)
    return (pq, num_local, den_local, kv_blocks, k_blocks)


def finish(pq, num_local, den_local, kv_blocks, k_blocks, prior_kv, prior_k):
    rows, count, span, heads, dim = pq.shape
    before_kv = jnp.cumsum(kv_blocks, axis=1) - kv_blocks + prior_kv[:, None]
    before_k = jnp.cumsum(k_blocks, axis=1) - k_blocks + prior_k[:, None]
    pq32 = pq.astype(jnp.float32)
    num = num_local + jnp.einsum(
        "rnihd,rnhde->rnihe", pq32, before_kv, precision=lax.Precision.HIGHEST
    )
    den = jnp.transpose(den_local, (0, 1, 3, 2)) + jnp.sum(pq32 * before_k[:, :, None], axis=-1)
    result = (num / den[..., None]).astype(jnp.bfloat16)
    return result.reshape(rows, count * span, heads * dim)


def split_qkv(qkv):
    phi_q = features(qkv[:, :, 0].astype(jnp.float32)).astype(jnp.bfloat16)
    phi_k = features(qkv[:, :, 1].astype(jnp.float32)).astype(jnp.bfloat16)
    return (phi_q, phi_k, qkv[:, :, 2])


def shards(frames_in, w_qkv, w_out):
    rows, tok_local, width = frames_in.shape
    head_dim = width // HEADS
    def project(w, count):
        out = jnp.einsum("rtd,de->ret", frames_in, w, preferred_element_type=jnp.float32)
        out = out.astype(jnp.bfloat16).reshape(rows, count, HEADS, head_dim, tok_local)
        return jnp.transpose(out, (0, 4, 1, 2, 3))

    keys_values = project(w_qkv[:, width:], 2)
    queries = project(w_qkv[:, :width], 1)
    phi_q = features(queries[:, :, 0].astype(jnp.float32)).astype(jnp.bfloat16)
    phi_k = features(keys_values[:, :, 0].astype(jnp.float32)).astype(jnp.bfloat16)
    values = keys_values[:, :, 1]
    pq, num_local, den_local, kv_blocks, k_blocks = block_terms(phi_q, phi_k, values, SPAN)
    total_kv = jnp.sum(kv_blocks, axis=1)[0]
    total_k = jnp.sum(k_blocks, axis=1)[0]
    lanes = 128
    dense = total_kv.reshape(HEADS, -1, lanes)
    rows_kv = dense.shape[1]
    norm = jnp.pad(total_k, ((0, 0), (0, lanes - total_k.shape[1])))[:, None]
    (own, other), (num_local, den_local) = entering(
        jnp.concatenate([dense, norm], axis=1), (num_local, den_local)
    )
    core = lax.axis_index("frm")
    half_heads = HEADS // 2

    def heads_of(prior, which):
        first = which * half_heads
        pick = lambda t, axis: lax.dynamic_slice_in_dim(t, first, half_heads, axis=axis)
        prior_kv = prior[:, :rows_kv].reshape((half_heads,) + total_kv.shape[1:])
        prior_k = prior[:, rows_kv, : total_k.shape[1]]
        heads_out = finish(
            pick(pq, 3), pick(num_local, 3), pick(den_local, 2),
            pick(kv_blocks, 2), pick(k_blocks, 2), prior_kv[None], prior_k[None],
        )
        rows_w = lax.dynamic_slice_in_dim(w_out, first * head_dim, half_heads * head_dim, axis=0)
        return jnp.einsum("rtd,de->rte", heads_out, rows_w, preferred_element_type=jnp.float32)

    out = heads_of(own, core) + heads_of(other, 1 - core)
    return out.astype(jnp.bfloat16)


def solution(mesh):
    sizes = [n for _, n in SEG_SPLIT]
    devices = mesh.devices.reshape(
        *sizes, mesh.shape["frm"], mesh.shape["rec"]
    )
    fine = Mesh(devices, tuple(name for name, _ in SEG_SPLIT) + ("frm", "rec"))
    in_specs = (P("rec", SCAN_AXES, None), P(), P())
    out_specs = P("rec", SCAN_AXES, None)
    return jax.shard_map(shards, mesh=fine, in_specs=in_specs, out_specs=out_specs, check_vma=False)
```

```python
import jax
import jax.numpy as jnp
from jax import lax
from jax.sharding import Mesh, PartitionSpec as P

HEADS = 16
SPAN = 256

SEG_SPLIT = (("seg_z", 8), ("seg_y", 4), ("seg_x", 2))
SCAN_AXES = ("seg_z", "seg_y", "seg_x", "frm")


def features(t):
    return jnp.where(t > 0.0, t + 1.0, jnp.exp(jnp.minimum(t, 0.0)))


def tmap(f, *trees):
    return jax.tree.map(f, *trees)


def send(tree, axis, pairs):
    return tmap(lambda t: lax.ppermute(t, axis, perm=pairs), tree)


def swap(tree, axis):
    return send(tree, axis, [(0, 1), (1, 0)])


def forward(n, s):
    return [(i, i + s) for i in range(n - s)]


def part(tree, index, count):
    def one(t):
        size = t.shape[0] // count
        return lax.dynamic_slice_in_dim(t, index * size, size, axis=0)

    return tmap(one, tree)


def ordered(mine, other, first):
    lo = tmap(lambda a, b: jnp.where(first, a, b), mine, other)
    hi = tmap(lambda a, b: jnp.where(first, b, a), mine, other)
    return lo, hi


def keep(tree, cond):
    return tmap(lambda a: jnp.where(cond, a, jnp.zeros_like(a)), tree)


def joined(lo, hi):
    return tmap(lambda a, b: jnp.concatenate([a, b], axis=0), lo, hi)


def cyclic(n, s):
    return [(i, (i + s) % n) for i in range(n)]


def entering(total, carry):
    core = lax.axis_index("frm")
    xh = lax.axis_index("seg_x")
    y = lax.axis_index("seg_y")
    z = lax.axis_index("seg_z")
    n_y = lax.axis_size("seg_y")
    n_z = lax.axis_size("seg_z")
    add = lambda a, b: tmap(jnp.add, a, b)
    own_c = part(total, core, 2)
    got_c = swap(part(total, 1 - core, 2), "frm")
    lo, hi = ordered(own_c, got_c, core == 0)
    chip = add(lo, hi)
    came = [part(chip, y, n_y)] + [
        send(part(chip, (y + s) % n_y, n_y), "seg_y", cyclic(n_y, s)) for s in range(1, n_y)
    ]
    column = came[0]
    for c in came[1:]:
        column = add(column, c)
    before_z = tmap(jnp.zeros_like, column)
    left = right = column
    lefts = []
    for r in range(1, n_z // 2 - 1):
        left = send(left, "seg_z", cyclic(n_z, 1))
        lefts.append(left)
        before_z = add(before_z, keep(left, z >= r))
    far = len(lefts)
    receiver = (z + far) % n_z
    onward = tmap(jnp.zeros_like, column)
    for k, piece in enumerate(lefts):
        onward = add(onward, keep(piece, receiver >= far + k + 1))
    before_z = add(before_z, send(onward, "seg_z", cyclic(n_z, far)))
    for r in range(1, n_z // 2):
        right = send(right, "seg_z", cyclic(n_z, -1))
        before_z = add(before_z, keep(right, z + r >= n_z))
    before_z, carry = lax.optimization_barrier((before_z, carry))

    def for_row(t):
        out = before_z
        for s, c in enumerate(came):
            out = add(out, keep(c, (y - s) % n_y < t))
        return out

    pieces = [for_row(y)] + [
        send(for_row((y + s) % n_y), "seg_y", cyclic(n_y, s)) for s in range(1, n_y)
    ]
    order = (y - jnp.arange(n_y)) % n_y
    mine = tmap(
        lambda *p: jnp.stack(p)[order].reshape((-1,) + p[0].shape[1:]),
        *pieces,
    )
    half = add(mine, swap(add(mine, keep(chip, xh == 0)), "seg_x"))
    got = swap(add(half, keep(own_c, core == 0)), "frm")
    own = tmap(lambda a, c: jnp.where(core == 0, a, a + c), half, got_c)
    return (own, got), carry


def block_terms(phi_q, phi_k, values, span):
    rows, length, heads, dim = phi_q.shape
    count = length // span
    pq = phi_q.reshape(rows, count, span, heads, dim)
    pk = phi_k.reshape(rows, count, span, heads, dim)
    vv = values.reshape(rows, count, span, heads, dim)
    scores = jnp.einsum("rnihd,rnjhd->rnhij", pq, pk, preferred_element_type=jnp.float32)
    causal = jnp.arange(span)[:, None] >= jnp.arange(span)[None, :]
    scores = jnp.where(causal, scores, 0.0)
    den_local = jnp.sum(scores, axis=-1)
    weights = scores.astype(jnp.bfloat16)
    num_local = jnp.einsum("rnhij,rnjhd->rnihd", weights, vv, preferred_element_type=jnp.float32)
    kv_blocks = jnp.einsum("rnjhd,rnjhe->rnhde", pk, vv, preferred_element_type=jnp.float32)
    k_blocks = jnp.sum(pk, axis=2, dtype=jnp.float32)
    return (pq, num_local, den_local, kv_blocks, k_blocks)


def finish(pq, num_local, den_local, kv_blocks, k_blocks, prior_kv, prior_k):
    rows, count, span, heads, dim = pq.shape
    before_kv = jnp.cumsum(kv_blocks, axis=1) - kv_blocks + prior_kv[:, None]
    before_k = jnp.cumsum(k_blocks, axis=1) - k_blocks + prior_k[:, None]
    pq32 = pq.astype(jnp.float32)
    num = num_local + jnp.einsum(
        "rnihd,rnhde->rnihe", pq32, before_kv, precision=lax.Precision.HIGHEST
    )
    den = jnp.transpose(den_local, (0, 1, 3, 2)) + jnp.sum(pq32 * before_k[:, :, None], axis=-1)
    result = (num / den[..., None]).astype(jnp.bfloat16)
    return result.reshape(rows, count * span, heads * dim)


def split_qkv(qkv):
    phi_q = features(qkv[:, :, 0].astype(jnp.float32)).astype(jnp.bfloat16)
    phi_k = features(qkv[:, :, 1].astype(jnp.float32)).astype(jnp.bfloat16)
    return (phi_q, phi_k, qkv[:, :, 2])


def shards(frames_in, w_qkv, w_out):
    rows, tok_local, width = frames_in.shape
    head_dim = width // HEADS
    def project(w, count):
        out = jnp.einsum("rtd,de->ret", frames_in, w, preferred_element_type=jnp.float32)
        out = out.astype(jnp.bfloat16).reshape(rows, count, HEADS, head_dim, tok_local)
        return jnp.transpose(out, (0, 4, 1, 2, 3))

    keys_values = project(w_qkv[:, width:], 2)
    queries = project(w_qkv[:, :width], 1)
    phi_q = features(queries[:, :, 0].astype(jnp.float32)).astype(jnp.bfloat16)
    phi_k = features(keys_values[:, :, 0].astype(jnp.float32)).astype(jnp.bfloat16)
    values = keys_values[:, :, 1]
    pq, num_local, den_local, kv_blocks, k_blocks = block_terms(phi_q, phi_k, values, SPAN)
    total_kv = jnp.sum(kv_blocks, axis=1)[0]
    total_k = jnp.sum(k_blocks, axis=1)[0]
    lanes = 128
    dense = total_kv.reshape(HEADS, -1, lanes)
    rows_kv = dense.shape[1]
    norm = jnp.pad(total_k, ((0, 0), (0, lanes - total_k.shape[1])))[:, None]
    (own, other), (num_local, den_local) = entering(
        jnp.concatenate([dense, norm], axis=1), (num_local, den_local)
    )
    core = lax.axis_index("frm")
    half_heads = HEADS // 2

    def heads_of(prior, which):
        first = which * half_heads
        pick = lambda t, axis: lax.dynamic_slice_in_dim(t, first, half_heads, axis=axis)
        prior_kv = prior[:, :rows_kv].reshape((half_heads,) + total_kv.shape[1:])
        prior_k = prior[:, rows_kv, : total_k.shape[1]]
        heads_out = finish(
            pick(pq, 3), pick(num_local, 3), pick(den_local, 2),
            pick(kv_blocks, 2), pick(k_blocks, 2), prior_kv[None], prior_k[None],
        )
        rows_w = lax.dynamic_slice_in_dim(w_out, first * head_dim, half_heads * head_dim, axis=0)
        return jnp.einsum("rtd,de->rte", heads_out, rows_w, preferred_element_type=jnp.float32)

    out = heads_of(own, core) + heads_of(other, 1 - core)
    return out.astype(jnp.bfloat16)


def solution(mesh):
    sizes = [n for _, n in SEG_SPLIT]
    devices = mesh.devices.reshape(
        *sizes, mesh.shape["frm"], mesh.shape["rec"]
    )
    fine = Mesh(devices, tuple(name for name, _ in SEG_SPLIT) + ("frm", "rec"))
    in_specs = (P("rec", SCAN_AXES, None), P(), P())
    out_specs = P("rec", SCAN_AXES, None)
    return jax.shard_map(shards, mesh=fine, in_specs=in_specs, out_specs=out_specs, check_vma=False)
```

```python
import jax
import jax.numpy as jnp
from jax import lax
from jax.sharding import Mesh, PartitionSpec as P

HEADS = 16
SPAN = 256

SEG_SPLIT = (("seg_z", 8), ("seg_y", 4), ("seg_x", 2))
SCAN_AXES = ("seg_z", "seg_y", "seg_x", "frm")


def features(t):
    return jnp.where(t > 0.0, t + 1.0, jnp.exp(jnp.minimum(t, 0.0)))


def tmap(f, *trees):
    return jax.tree.map(f, *trees)


def send(tree, axis, pairs):
    return tmap(lambda t: lax.ppermute(t, axis, perm=pairs), tree)


def swap(tree, axis):
    return send(tree, axis, [(0, 1), (1, 0)])


def forward(n, s):
    return [(i, i + s) for i in range(n - s)]


def part(tree, index, count):
    def one(t):
        size = t.shape[0] // count
        return lax.dynamic_slice_in_dim(t, index * size, size, axis=0)

    return tmap(one, tree)


def ordered(mine, other, first):
    lo = tmap(lambda a, b: jnp.where(first, a, b), mine, other)
    hi = tmap(lambda a, b: jnp.where(first, b, a), mine, other)
    return lo, hi


def keep(tree, cond):
    return tmap(lambda a: jnp.where(cond, a, jnp.zeros_like(a)), tree)


def joined(lo, hi):
    return tmap(lambda a, b: jnp.concatenate([a, b], axis=0), lo, hi)


def cyclic(n, s):
    return [(i, (i + s) % n) for i in range(n)]


def entering(total, carry):
    core = lax.axis_index("frm")
    xh = lax.axis_index("seg_x")
    y = lax.axis_index("seg_y")
    z = lax.axis_index("seg_z")
    n_y = lax.axis_size("seg_y")
    n_z = lax.axis_size("seg_z")
    add = lambda a, b: tmap(jnp.add, a, b)
    own_c = part(total, core, 2)
    got_c = swap(part(total, 1 - core, 2), "frm")
    lo, hi = ordered(own_c, got_c, core == 0)
    chip = add(lo, hi)
    came = [part(chip, y, n_y)] + [
        send(part(chip, (y + s) % n_y, n_y), "seg_y", cyclic(n_y, s)) for s in range(1, n_y)
    ]
    column = came[0]
    for c in came[1:]:
        column = add(column, c)
    assert n_z == 8
    left = send(column, "seg_z", cyclic(n_z, 1))
    right = send(column, "seg_z", cyclic(n_z, -1))
    before_z = add(keep(left, z >= 1), keep(right, z + 1 >= n_z))
    to = lambda s: (z + s) % n_z
    two = send(keep(column, to(2) >= 2), "seg_z", cyclic(n_z, 2))
    three = add(keep(column, to(3) >= 3), keep(left, to(3) >= 4))
    three = send(three, "seg_z", cyclic(n_z, 3))
    back = add(keep(column, to(-2) + 2 >= n_z), keep(right, to(-2) + 3 >= n_z))
    back = send(back, "seg_z", cyclic(n_z, -2))
    before_z = add(before_z, add(two, add(three, back)))
    before_z, carry = lax.optimization_barrier((before_z, carry))

    def for_row(t):
        out = before_z
        for s, c in enumerate(came):
            out = add(out, keep(c, (y - s) % n_y < t))
        return out

    pieces = [for_row(y)] + [
        send(for_row((y + s) % n_y), "seg_y", cyclic(n_y, s)) for s in range(1, n_y)
    ]
    order = (y - jnp.arange(n_y)) % n_y
    mine = tmap(
        lambda *p: jnp.stack(p)[order].reshape((-1,) + p[0].shape[1:]),
        *pieces,
    )
    half = add(mine, swap(add(mine, keep(chip, xh == 0)), "seg_x"))
    got = swap(add(half, keep(own_c, core == 0)), "frm")
    own = tmap(lambda a, c: jnp.where(core == 0, a, a + c), half, got_c)
    return (own, got), carry


def block_terms(phi_q, phi_k, values, span):
    rows, length, heads, dim = phi_q.shape
    count = length // span
    pq = phi_q.reshape(rows, count, span, heads, dim)
    pk = phi_k.reshape(rows, count, span, heads, dim)
    vv = values.reshape(rows, count, span, heads, dim)
    scores = jnp.einsum("rnihd,rnjhd->rnhij", pq, pk, preferred_element_type=jnp.float32)
    causal = jnp.arange(span)[:, None] >= jnp.arange(span)[None, :]
    scores = jnp.where(causal, scores, 0.0)
    den_local = jnp.sum(scores, axis=-1)
    weights = scores.astype(jnp.bfloat16)
    num_local = jnp.einsum("rnhij,rnjhd->rnihd", weights, vv, preferred_element_type=jnp.float32)
    kv_blocks = jnp.einsum("rnjhd,rnjhe->rnhde", pk, vv, preferred_element_type=jnp.float32)
    k_blocks = jnp.sum(pk, axis=2, dtype=jnp.float32)
    return (pq, num_local, den_local, kv_blocks, k_blocks)


def finish(pq, num_local, den_local, kv_blocks, k_blocks, prior_kv, prior_k):
    rows, count, span, heads, dim = pq.shape
    before_kv = jnp.cumsum(kv_blocks, axis=1) - kv_blocks + prior_kv[:, None]
    before_k = jnp.cumsum(k_blocks, axis=1) - k_blocks + prior_k[:, None]
    pq32 = pq.astype(jnp.float32)
    num = num_local + jnp.einsum(
        "rnihd,rnhde->rnihe", pq32, before_kv, precision=lax.Precision.HIGHEST
    )
    den = jnp.transpose(den_local, (0, 1, 3, 2)) + jnp.sum(pq32 * before_k[:, :, None], axis=-1)
    result = (num / den[..., None]).astype(jnp.bfloat16)
    return result.reshape(rows, count * span, heads * dim)


def split_qkv(qkv):
    phi_q = features(qkv[:, :, 0].astype(jnp.float32)).astype(jnp.bfloat16)
    phi_k = features(qkv[:, :, 1].astype(jnp.float32)).astype(jnp.bfloat16)
    return (phi_q, phi_k, qkv[:, :, 2])


def shards(frames_in, w_qkv, w_out):
    rows, tok_local, width = frames_in.shape
    head_dim = width // HEADS
    def project(w, count):
        out = jnp.einsum("rtd,de->ret", frames_in, w, preferred_element_type=jnp.float32)
        out = out.astype(jnp.bfloat16).reshape(rows, count, HEADS, head_dim, tok_local)
        return jnp.transpose(out, (0, 4, 1, 2, 3))

    keys_values = project(w_qkv[:, width:], 2)
    queries = project(w_qkv[:, :width], 1)
    phi_q = features(queries[:, :, 0].astype(jnp.float32)).astype(jnp.bfloat16)
    phi_k = features(keys_values[:, :, 0].astype(jnp.float32)).astype(jnp.bfloat16)
    values = keys_values[:, :, 1]
    pq, num_local, den_local, kv_blocks, k_blocks = block_terms(phi_q, phi_k, values, SPAN)
    total_kv = jnp.sum(kv_blocks, axis=1)[0]
    total_k = jnp.sum(k_blocks, axis=1)[0]
    lanes = 128
    dense = total_kv.reshape(HEADS, -1, lanes)
    rows_kv = dense.shape[1]
    norm = jnp.pad(total_k, ((0, 0), (0, lanes - total_k.shape[1])))[:, None]
    (own, other), (num_local, den_local) = entering(
        jnp.concatenate([dense, norm], axis=1), (num_local, den_local)
    )
    core = lax.axis_index("frm")
    half_heads = HEADS // 2

    def heads_of(prior, which):
        first = which * half_heads
        pick = lambda t, axis: lax.dynamic_slice_in_dim(t, first, half_heads, axis=axis)
        prior_kv = prior[:, :rows_kv].reshape((half_heads,) + total_kv.shape[1:])
        prior_k = prior[:, rows_kv, : total_k.shape[1]]
        heads_out = finish(
            pick(pq, 3), pick(num_local, 3), pick(den_local, 2),
            pick(kv_blocks, 2), pick(k_blocks, 2), prior_kv[None], prior_k[None],
        )
        rows_w = lax.dynamic_slice_in_dim(w_out, first * head_dim, half_heads * head_dim, axis=0)
        return jnp.einsum("rtd,de->rte", heads_out, rows_w, preferred_element_type=jnp.float32)

    out = heads_of(own, core) + heads_of(other, 1 - core)
    return out.astype(jnp.bfloat16)


def solution(mesh):
    sizes = [n for _, n in SEG_SPLIT]
    devices = mesh.devices.reshape(
        *sizes, mesh.shape["frm"], mesh.shape["rec"]
    )
    fine = Mesh(devices, tuple(name for name, _ in SEG_SPLIT) + ("frm", "rec"))
    in_specs = (P("rec", SCAN_AXES, None), P(), P())
    out_specs = P("rec", SCAN_AXES, None)
    return jax.shard_map(shards, mesh=fine, in_specs=in_specs, out_specs=out_specs, check_vma=False)
```

```python
import jax
import jax.numpy as jnp
from jax import lax
from jax.sharding import Mesh, PartitionSpec as P

HEADS = 16
SPAN = 256

SEG_SPLIT = (("seg_z", 8), ("seg_y", 4), ("seg_x", 2))
SCAN_AXES = ("seg_z", "seg_y", "seg_x", "frm")


def features(t):
    return jnp.where(t > 0.0, t + 1.0, jnp.exp(jnp.minimum(t, 0.0)))


def tmap(f, *trees):
    return jax.tree.map(f, *trees)


def send(tree, axis, pairs):
    return tmap(lambda t: lax.ppermute(t, axis, perm=pairs), tree)


def swap(tree, axis):
    return send(tree, axis, [(0, 1), (1, 0)])


def forward(n, s):
    return [(i, i + s) for i in range(n - s)]


def part(tree, index, count):
    def one(t):
        size = t.shape[0] // count
        return lax.dynamic_slice_in_dim(t, index * size, size, axis=0)

    return tmap(one, tree)


def ordered(mine, other, first):
    lo = tmap(lambda a, b: jnp.where(first, a, b), mine, other)
    hi = tmap(lambda a, b: jnp.where(first, b, a), mine, other)
    return lo, hi


def keep(tree, cond):
    return tmap(lambda a: jnp.where(cond, a, jnp.zeros_like(a)), tree)


def joined(lo, hi):
    return tmap(lambda a, b: jnp.concatenate([a, b], axis=0), lo, hi)


def cyclic(n, s):
    return [(i, (i + s) % n) for i in range(n)]


def entering(total, carry):
    core = lax.axis_index("frm")
    xh = lax.axis_index("seg_x")
    y = lax.axis_index("seg_y")
    z = lax.axis_index("seg_z")
    n_y = lax.axis_size("seg_y")
    n_z = lax.axis_size("seg_z")
    add = lambda a, b: tmap(jnp.add, a, b)
    own_c = part(total, core, 2)
    got_c = swap(part(total, 1 - core, 2), "frm")
    lo, hi = ordered(own_c, got_c, core == 0)
    chip = add(lo, hi)
    came = [part(chip, y, n_y)] + [
        send(part(chip, (y + s) % n_y, n_y), "seg_y", cyclic(n_y, s)) for s in range(1, n_y)
    ]
    column = came[0]
    for c in came[1:]:
        column = add(column, c)
    assert n_z == 8
    left = send(column, "seg_z", cyclic(n_z, 1))
    far = send(column, "seg_z", cyclic(n_z, 2))
    right = send(column, "seg_z", cyclic(n_z, -1))
    before_z = add(add(keep(left, z >= 1), keep(far, z >= 2)), keep(right, z + 1 >= n_z))
    to = lambda s: (z + s) % n_z
    onward = add(keep(left, to(2) >= 3), keep(far, to(2) >= 4))
    onward = send(onward, "seg_z", cyclic(n_z, 2))
    back = add(keep(column, to(-2) + 2 >= n_z), keep(right, to(-2) + 3 >= n_z))
    back = send(back, "seg_z", cyclic(n_z, -2))
    before_z = add(before_z, add(onward, back))
    before_z, carry = lax.optimization_barrier((before_z, carry))

    def for_row(t):
        out = before_z
        for s, c in enumerate(came):
            out = add(out, keep(c, (y - s) % n_y < t))
        return out

    pieces = [for_row(y)] + [
        send(for_row((y + s) % n_y), "seg_y", cyclic(n_y, s)) for s in range(1, n_y)
    ]
    order = (y - jnp.arange(n_y)) % n_y
    mine = tmap(
        lambda *p: jnp.stack(p)[order].reshape((-1,) + p[0].shape[1:]),
        *pieces,
    )
    half = add(mine, swap(add(mine, keep(chip, xh == 0)), "seg_x"))
    got = swap(add(half, keep(own_c, core == 0)), "frm")
    own = tmap(lambda a, c: jnp.where(core == 0, a, a + c), half, got_c)
    return (own, got), carry


def block_terms(phi_q, phi_k, values, span):
    rows, length, heads, dim = phi_q.shape
    count = length // span
    pq = phi_q.reshape(rows, count, span, heads, dim)
    pk = phi_k.reshape(rows, count, span, heads, dim)
    vv = values.reshape(rows, count, span, heads, dim)
    scores = jnp.einsum("rnihd,rnjhd->rnhij", pq, pk, preferred_element_type=jnp.float32)
    causal = jnp.arange(span)[:, None] >= jnp.arange(span)[None, :]
    scores = jnp.where(causal, scores, 0.0)
    den_local = jnp.sum(scores, axis=-1)
    weights = scores.astype(jnp.bfloat16)
    num_local = jnp.einsum("rnhij,rnjhd->rnihd", weights, vv, preferred_element_type=jnp.float32)
    kv_blocks = jnp.einsum("rnjhd,rnjhe->rnhde", pk, vv, preferred_element_type=jnp.float32)
    k_blocks = jnp.sum(pk, axis=2, dtype=jnp.float32)
    return (pq, num_local, den_local, kv_blocks, k_blocks)


def finish(pq, num_local, den_local, kv_blocks, k_blocks, prior_kv, prior_k):
    rows, count, span, heads, dim = pq.shape
    before_kv = jnp.cumsum(kv_blocks, axis=1) - kv_blocks + prior_kv[:, None]
    before_k = jnp.cumsum(k_blocks, axis=1) - k_blocks + prior_k[:, None]
    pq32 = pq.astype(jnp.float32)
    num = num_local + jnp.einsum(
        "rnihd,rnhde->rnihe", pq32, before_kv, precision=lax.Precision.HIGHEST
    )
    den = jnp.transpose(den_local, (0, 1, 3, 2)) + jnp.sum(pq32 * before_k[:, :, None], axis=-1)
    result = (num / den[..., None]).astype(jnp.bfloat16)
    return result.reshape(rows, count * span, heads * dim)


def split_qkv(qkv):
    phi_q = features(qkv[:, :, 0].astype(jnp.float32)).astype(jnp.bfloat16)
    phi_k = features(qkv[:, :, 1].astype(jnp.float32)).astype(jnp.bfloat16)
    return (phi_q, phi_k, qkv[:, :, 2])


def shards(frames_in, w_qkv, w_out):
    rows, tok_local, width = frames_in.shape
    head_dim = width // HEADS
    def project(w, count):
        out = jnp.einsum("rtd,de->ret", frames_in, w, preferred_element_type=jnp.float32)
        out = out.astype(jnp.bfloat16).reshape(rows, count, HEADS, head_dim, tok_local)
        return jnp.transpose(out, (0, 4, 1, 2, 3))

    keys_values = project(w_qkv[:, width:], 2)
    queries = project(w_qkv[:, :width], 1)
    phi_q = features(queries[:, :, 0].astype(jnp.float32)).astype(jnp.bfloat16)
    phi_k = features(keys_values[:, :, 0].astype(jnp.float32)).astype(jnp.bfloat16)
    values = keys_values[:, :, 1]
    pq, num_local, den_local, kv_blocks, k_blocks = block_terms(phi_q, phi_k, values, SPAN)
    total_kv = jnp.sum(kv_blocks, axis=1)[0]
    total_k = jnp.sum(k_blocks, axis=1)[0]
    lanes = 128
    dense = total_kv.reshape(HEADS, -1, lanes)
    rows_kv = dense.shape[1]
    norm = jnp.pad(total_k, ((0, 0), (0, lanes - total_k.shape[1])))[:, None]
    (own, other), (num_local, den_local) = entering(
        jnp.concatenate([dense, norm], axis=1), (num_local, den_local)
    )
    core = lax.axis_index("frm")
    half_heads = HEADS // 2

    def heads_of(prior, which):
        first = which * half_heads
        pick = lambda t, axis: lax.dynamic_slice_in_dim(t, first, half_heads, axis=axis)
        prior_kv = prior[:, :rows_kv].reshape((half_heads,) + total_kv.shape[1:])
        prior_k = prior[:, rows_kv, : total_k.shape[1]]
        heads_out = finish(
            pick(pq, 3), pick(num_local, 3), pick(den_local, 2),
            pick(kv_blocks, 2), pick(k_blocks, 2), prior_kv[None], prior_k[None],
        )
        rows_w = lax.dynamic_slice_in_dim(w_out, first * head_dim, half_heads * head_dim, axis=0)
        return jnp.einsum("rtd,de->rte", heads_out, rows_w, preferred_element_type=jnp.float32)

    out = heads_of(own, core) + heads_of(other, 1 - core)
    return out.astype(jnp.bfloat16)


def solution(mesh):
    sizes = [n for _, n in SEG_SPLIT]
    devices = mesh.devices.reshape(
        *sizes, mesh.shape["frm"], mesh.shape["rec"]
    )
    fine = Mesh(devices, tuple(name for name, _ in SEG_SPLIT) + ("frm", "rec"))
    in_specs = (P("rec", SCAN_AXES, None), P(), P())
    out_specs = P("rec", SCAN_AXES, None)
    return jax.shard_map(shards, mesh=fine, in_specs=in_specs, out_specs=out_specs, check_vma=False)
```

```python
import jax
import jax.numpy as jnp
from jax import lax
from jax.sharding import Mesh, PartitionSpec as P

HEADS = 16
SPAN = 256

SEG_SPLIT = (("seg_z", 8), ("seg_y", 4), ("seg_x", 2))
SCAN_AXES = ("seg_z", "seg_y", "seg_x", "frm")


def features(t):
    return jnp.where(t > 0.0, t + 1.0, jnp.exp(jnp.minimum(t, 0.0)))


def tmap(f, *trees):
    return jax.tree.map(f, *trees)


def send(tree, axis, pairs):
    return tmap(lambda t: lax.ppermute(t, axis, perm=pairs), tree)


def swap(tree, axis):
    return send(tree, axis, [(0, 1), (1, 0)])


def forward(n, s):
    return [(i, i + s) for i in range(n - s)]


def part(tree, index, count):
    def one(t):
        size = t.shape[0] // count
        return lax.dynamic_slice_in_dim(t, index * size, size, axis=0)

    return tmap(one, tree)


def ordered(mine, other, first):
    lo = tmap(lambda a, b: jnp.where(first, a, b), mine, other)
    hi = tmap(lambda a, b: jnp.where(first, b, a), mine, other)
    return lo, hi


def keep(tree, cond):
    return tmap(lambda a: jnp.where(cond, a, jnp.zeros_like(a)), tree)


def joined(lo, hi):
    return tmap(lambda a, b: jnp.concatenate([a, b], axis=0), lo, hi)


def cyclic(n, s):
    return [(i, (i + s) % n) for i in range(n)]


def entering(total, carry):
    core = lax.axis_index("frm")
    xh = lax.axis_index("seg_x")
    y = lax.axis_index("seg_y")
    z = lax.axis_index("seg_z")
    n_y = lax.axis_size("seg_y")
    n_z = lax.axis_size("seg_z")
    add = lambda a, b: tmap(jnp.add, a, b)
    own_c = part(total, core, 2)
    got_c = swap(part(total, 1 - core, 2), "frm")
    lo, hi = ordered(own_c, got_c, core == 0)
    chip = add(lo, hi)
    came = [part(chip, y, n_y)] + [
        send(part(chip, (y + s) % n_y, n_y), "seg_y", cyclic(n_y, s)) for s in range(1, n_y)
    ]
    column = came[0]
    for c in came[1:]:
        column = add(column, c)
    assert n_z == 8
    left = send(column, "seg_z", cyclic(n_z, 1))
    right = send(column, "seg_z", cyclic(n_z, -1))
    before_z = add(keep(left, z >= 1), keep(right, z + 1 >= n_z))
    to = lambda s: (z + s) % n_z
    two = send(keep(column, to(2) >= 2), "seg_z", cyclic(n_z, 2))
    three = add(keep(column, to(3) >= 3), keep(left, to(3) >= 4))
    three = send(three, "seg_z", cyclic(n_z, 3))
    back = add(keep(column, to(-2) + 2 >= n_z), keep(right, to(-2) + 3 >= n_z))
    back = send(back, "seg_z", cyclic(n_z, -2))
    before_z = add(before_z, add(two, add(three, back)))
    before_z, carry = lax.optimization_barrier((before_z, carry))

    def for_row(t):
        out = before_z
        for s, c in enumerate(came):
            out = add(out, keep(c, (y - s) % n_y < t))
        return out

    pieces = [for_row(y)] + [
        send(for_row((y + s) % n_y), "seg_y", cyclic(n_y, s)) for s in range(1, n_y)
    ]
    def placed(j):
        out = keep(pieces[0], y == j)
        for s in range(1, n_y):
            out = add(out, keep(pieces[s], (y - s) % n_y == j))
        return out

    mine = tmap(lambda *p: jnp.concatenate(p, axis=0), *[placed(j) for j in range(n_y)])
    half = add(mine, swap(add(mine, keep(chip, xh == 0)), "seg_x"))
    got = swap(add(half, keep(own_c, core == 0)), "frm")
    own = tmap(lambda a, c: jnp.where(core == 0, a, a + c), half, got_c)
    return (own, got), carry


def block_terms(phi_q, phi_k, values, span):
    rows, length, heads, dim = phi_q.shape
    count = length // span
    pq = phi_q.reshape(rows, count, span, heads, dim)
    pk = phi_k.reshape(rows, count, span, heads, dim)
    vv = values.reshape(rows, count, span, heads, dim)
    scores = jnp.einsum("rnihd,rnjhd->rnhij", pq, pk, preferred_element_type=jnp.float32)
    causal = jnp.arange(span)[:, None] >= jnp.arange(span)[None, :]
    scores = jnp.where(causal, scores, 0.0)
    den_local = jnp.sum(scores, axis=-1)
    weights = scores.astype(jnp.bfloat16)
    num_local = jnp.einsum("rnhij,rnjhd->rnihd", weights, vv, preferred_element_type=jnp.float32)
    kv_blocks = jnp.einsum("rnjhd,rnjhe->rnhde", pk, vv, preferred_element_type=jnp.float32)
    k_blocks = jnp.sum(pk, axis=2, dtype=jnp.float32)
    return (pq, num_local, den_local, kv_blocks, k_blocks)


def finish(pq, num_local, den_local, kv_blocks, k_blocks, prior_kv, prior_k):
    rows, count, span, heads, dim = pq.shape
    before_kv = jnp.cumsum(kv_blocks, axis=1) - kv_blocks + prior_kv[:, None]
    before_k = jnp.cumsum(k_blocks, axis=1) - k_blocks + prior_k[:, None]
    pq32 = pq.astype(jnp.float32)
    num = num_local + jnp.einsum(
        "rnihd,rnhde->rnihe", pq32, before_kv, precision=lax.Precision.HIGHEST
    )
    den = jnp.transpose(den_local, (0, 1, 3, 2)) + jnp.sum(pq32 * before_k[:, :, None], axis=-1)
    result = (num / den[..., None]).astype(jnp.bfloat16)
    return result.reshape(rows, count * span, heads * dim)


def split_qkv(qkv):
    phi_q = features(qkv[:, :, 0].astype(jnp.float32)).astype(jnp.bfloat16)
    phi_k = features(qkv[:, :, 1].astype(jnp.float32)).astype(jnp.bfloat16)
    return (phi_q, phi_k, qkv[:, :, 2])


def shards(frames_in, w_qkv, w_out):
    rows, tok_local, width = frames_in.shape
    head_dim = width // HEADS
    def project(w, count):
        out = jnp.einsum("rtd,de->ret", frames_in, w, preferred_element_type=jnp.float32)
        out = out.astype(jnp.bfloat16).reshape(rows, count, HEADS, head_dim, tok_local)
        return jnp.transpose(out, (0, 4, 1, 2, 3))

    keys_values = project(w_qkv[:, width:], 2)
    queries = project(w_qkv[:, :width], 1)
    phi_q = features(queries[:, :, 0].astype(jnp.float32)).astype(jnp.bfloat16)
    phi_k = features(keys_values[:, :, 0].astype(jnp.float32)).astype(jnp.bfloat16)
    values = keys_values[:, :, 1]
    pq, num_local, den_local, kv_blocks, k_blocks = block_terms(phi_q, phi_k, values, SPAN)
    total_kv = jnp.sum(kv_blocks, axis=1)[0]
    total_k = jnp.sum(k_blocks, axis=1)[0]
    lanes = 128
    dense = total_kv.reshape(HEADS, -1, lanes)
    rows_kv = dense.shape[1]
    norm = jnp.pad(total_k, ((0, 0), (0, lanes - total_k.shape[1])))[:, None]
    (own, other), (num_local, den_local) = entering(
        jnp.concatenate([dense, norm], axis=1), (num_local, den_local)
    )
    core = lax.axis_index("frm")
    half_heads = HEADS // 2

    def heads_of(prior, which):
        first = which * half_heads
        pick = lambda t, axis: lax.dynamic_slice_in_dim(t, first, half_heads, axis=axis)
        prior_kv = prior[:, :rows_kv].reshape((half_heads,) + total_kv.shape[1:])
        prior_k = prior[:, rows_kv, : total_k.shape[1]]
        heads_out = finish(
            pick(pq, 3), pick(num_local, 3), pick(den_local, 2),
            pick(kv_blocks, 2), pick(k_blocks, 2), prior_kv[None], prior_k[None],
        )
        rows_w = lax.dynamic_slice_in_dim(w_out, first * head_dim, half_heads * head_dim, axis=0)
        return jnp.einsum("rtd,de->rte", heads_out, rows_w, preferred_element_type=jnp.float32)

    out = heads_of(own, core) + heads_of(other, 1 - core)
    return out.astype(jnp.bfloat16)


def solution(mesh):
    sizes = [n for _, n in SEG_SPLIT]
    devices = mesh.devices.reshape(
        *sizes, mesh.shape["frm"], mesh.shape["rec"]
    )
    fine = Mesh(devices, tuple(name for name, _ in SEG_SPLIT) + ("frm", "rec"))
    in_specs = (P("rec", SCAN_AXES, None), P(), P())
    out_specs = P("rec", SCAN_AXES, None)
    return jax.shard_map(shards, mesh=fine, in_specs=in_specs, out_specs=out_specs, check_vma=False)
```

```python
import jax
import jax.numpy as jnp
from jax import lax
from jax.sharding import Mesh, PartitionSpec as P

HEADS = 16
SPAN = 256

SEG_SPLIT = (("seg_z", 8), ("seg_y", 4), ("seg_x", 2))
SCAN_AXES = ("seg_z", "seg_y", "seg_x", "frm")


def features(t):
    return jnp.where(t > 0.0, t + 1.0, jnp.exp(jnp.minimum(t, 0.0)))


def tmap(f, *trees):
    return jax.tree.map(f, *trees)


def send(tree, axis, pairs):
    return tmap(lambda t: lax.ppermute(t, axis, perm=pairs), tree)


def swap(tree, axis):
    return send(tree, axis, [(0, 1), (1, 0)])


def forward(n, s):
    return [(i, i + s) for i in range(n - s)]


def part(tree, index, count):
    def one(t):
        size = t.shape[0] // count
        return lax.dynamic_slice_in_dim(t, index * size, size, axis=0)

    return tmap(one, tree)


def ordered(mine, other, first):
    lo = tmap(lambda a, b: jnp.where(first, a, b), mine, other)
    hi = tmap(lambda a, b: jnp.where(first, b, a), mine, other)
    return lo, hi


def keep(tree, cond):
    return tmap(lambda a: jnp.where(cond, a, jnp.zeros_like(a)), tree)


def joined(lo, hi):
    return tmap(lambda a, b: jnp.concatenate([a, b], axis=0), lo, hi)


def cyclic(n, s):
    return [(i, (i + s) % n) for i in range(n)]


def entering(total, carry, late, use_late):
    core = lax.axis_index("frm")
    xh = lax.axis_index("seg_x")
    y = lax.axis_index("seg_y")
    z = lax.axis_index("seg_z")
    n_y = lax.axis_size("seg_y")
    n_z = lax.axis_size("seg_z")
    add = lambda a, b: tmap(jnp.add, a, b)
    own_c = part(total, core, 2)
    got_c = swap(part(total, 1 - core, 2), "frm")
    lo, hi = ordered(own_c, got_c, core == 0)
    chip = add(lo, hi)
    came = [part(chip, y, n_y)] + [
        send(part(chip, (y + s) % n_y, n_y), "seg_y", cyclic(n_y, s)) for s in range(1, n_y)
    ]
    column = came[0]
    for c in came[1:]:
        column = add(column, c)
    column, late = lax.optimization_barrier((column, late))
    carry = use_late(late, carry)
    assert n_z == 8
    left = send(column, "seg_z", cyclic(n_z, 1))
    right = send(column, "seg_z", cyclic(n_z, -1))
    before_z = add(keep(left, z >= 1), keep(right, z + 1 >= n_z))
    to = lambda s: (z + s) % n_z
    two = send(keep(column, to(2) >= 2), "seg_z", cyclic(n_z, 2))
    three = add(keep(column, to(3) >= 3), keep(left, to(3) >= 4))
    three = send(three, "seg_z", cyclic(n_z, 3))
    back = add(keep(column, to(-2) + 2 >= n_z), keep(right, to(-2) + 3 >= n_z))
    back = send(back, "seg_z", cyclic(n_z, -2))
    before_z = add(before_z, add(two, add(three, back)))
    before_z, carry = lax.optimization_barrier((before_z, carry))

    def for_row(t):
        out = before_z
        for s, c in enumerate(came):
            out = add(out, keep(c, (y - s) % n_y < t))
        return out

    pieces = [for_row(y)] + [
        send(for_row((y + s) % n_y), "seg_y", cyclic(n_y, s)) for s in range(1, n_y)
    ]
    order = (y - jnp.arange(n_y)) % n_y
    mine = tmap(
        lambda *p: jnp.stack(p)[order].reshape((-1,) + p[0].shape[1:]),
        *pieces,
    )
    half = add(mine, swap(add(mine, keep(chip, xh == 0)), "seg_x"))
    got = swap(add(half, keep(own_c, core == 0)), "frm")
    own = tmap(lambda a, c: jnp.where(core == 0, a, a + c), half, got_c)
    return (own, got), carry


def block_terms(phi_q, phi_k, values, span):
    rows, length, heads, dim = phi_q.shape
    count = length // span
    pq = phi_q.reshape(rows, count, span, heads, dim)
    pk = phi_k.reshape(rows, count, span, heads, dim)
    vv = values.reshape(rows, count, span, heads, dim)
    scores = jnp.einsum("rnihd,rnjhd->rnhij", pq, pk, preferred_element_type=jnp.float32)
    causal = jnp.arange(span)[:, None] >= jnp.arange(span)[None, :]
    scores = jnp.where(causal, scores, 0.0)
    den_local = jnp.sum(scores, axis=-1)
    weights = scores.astype(jnp.bfloat16)
    num_local = jnp.einsum("rnhij,rnjhd->rnihd", weights, vv, preferred_element_type=jnp.float32)
    kv_blocks = jnp.einsum("rnjhd,rnjhe->rnhde", pk, vv, preferred_element_type=jnp.float32)
    k_blocks = jnp.sum(pk, axis=2, dtype=jnp.float32)
    return (pq, num_local, den_local, kv_blocks, k_blocks)


def finish(pq, num_local, den_local, kv_blocks, k_blocks, prior_kv, prior_k):
    rows, count, span, heads, dim = pq.shape
    before_kv = jnp.cumsum(kv_blocks, axis=1) - kv_blocks + prior_kv[:, None]
    before_k = jnp.cumsum(k_blocks, axis=1) - k_blocks + prior_k[:, None]
    pq32 = pq.astype(jnp.float32)
    num = num_local + jnp.einsum(
        "rnihd,rnhde->rnihe", pq32, before_kv, precision=lax.Precision.HIGHEST
    )
    den = jnp.transpose(den_local, (0, 1, 3, 2)) + jnp.sum(pq32 * before_k[:, :, None], axis=-1)
    result = (num / den[..., None]).astype(jnp.bfloat16)
    return result.reshape(rows, count * span, heads * dim)


def split_qkv(qkv):
    phi_q = features(qkv[:, :, 0].astype(jnp.float32)).astype(jnp.bfloat16)
    phi_k = features(qkv[:, :, 1].astype(jnp.float32)).astype(jnp.bfloat16)
    return (phi_q, phi_k, qkv[:, :, 2])


def shards(frames_in, w_qkv, w_out):
    rows, tok_local, width = frames_in.shape
    head_dim = width // HEADS
    def project(w, count):
        out = jnp.einsum("rtd,de->ret", frames_in, w, preferred_element_type=jnp.float32)
        out = out.astype(jnp.bfloat16).reshape(rows, count, HEADS, head_dim, tok_local)
        return jnp.transpose(out, (0, 4, 1, 2, 3))

    keys_values = project(w_qkv[:, width:], 2)
    phi_k = features(keys_values[:, :, 0].astype(jnp.float32)).astype(jnp.bfloat16)
    values = keys_values[:, :, 1]
    kv_blocks = jnp.einsum(
        "rnjhd,rnjhe->rnhde",
        phi_k.reshape(rows, -1, SPAN, HEADS, head_dim),
        values.reshape(rows, -1, SPAN, HEADS, head_dim),
        preferred_element_type=jnp.float32,
    )
    k_blocks = jnp.sum(phi_k.reshape(rows, -1, SPAN, HEADS, head_dim), axis=2, dtype=jnp.float32)

    def local(frames, _):
        queries = jnp.einsum("rtd,de->ret", frames, w_qkv[:, :width], preferred_element_type=jnp.float32)
        queries = queries.astype(jnp.bfloat16).reshape(rows, 1, HEADS, head_dim, tok_local)
        queries = jnp.transpose(queries, (0, 4, 1, 2, 3))
        phi_q = features(queries[:, :, 0].astype(jnp.float32)).astype(jnp.bfloat16)
        pq, num_local, den_local, _, _ = block_terms(phi_q, phi_k, values, SPAN)
        return pq, num_local, den_local

    total_kv = jnp.sum(kv_blocks, axis=1)[0]
    total_k = jnp.sum(k_blocks, axis=1)[0]
    lanes = 128
    dense = total_kv.reshape(HEADS, -1, lanes)
    rows_kv = dense.shape[1]
    norm = jnp.pad(total_k, ((0, 0), (0, lanes - total_k.shape[1])))[:, None]
    (own, other), (pq, num_local, den_local) = entering(
        jnp.concatenate([dense, norm], axis=1), None, frames_in, local
    )
    core = lax.axis_index("frm")
    half_heads = HEADS // 2

    def heads_of(prior, which):
        first = which * half_heads
        pick = lambda t, axis: lax.dynamic_slice_in_dim(t, first, half_heads, axis=axis)
        prior_kv = prior[:, :rows_kv].reshape((half_heads,) + total_kv.shape[1:])
        prior_k = prior[:, rows_kv, : total_k.shape[1]]
        heads_out = finish(
            pick(pq, 3), pick(num_local, 3), pick(den_local, 2),
            pick(kv_blocks, 2), pick(k_blocks, 2), prior_kv[None], prior_k[None],
        )
        rows_w = lax.dynamic_slice_in_dim(w_out, first * head_dim, half_heads * head_dim, axis=0)
        return jnp.einsum("rtd,de->rte", heads_out, rows_w, preferred_element_type=jnp.float32)

    out = heads_of(own, core) + heads_of(other, 1 - core)
    return out.astype(jnp.bfloat16)


def solution(mesh):
    sizes = [n for _, n in SEG_SPLIT]
    devices = mesh.devices.reshape(
        *sizes, mesh.shape["frm"], mesh.shape["rec"]
    )
    fine = Mesh(devices, tuple(name for name, _ in SEG_SPLIT) + ("frm", "rec"))
    in_specs = (P("rec", SCAN_AXES, None), P(), P())
    out_specs = P("rec", SCAN_AXES, None)
    return jax.shard_map(shards, mesh=fine, in_specs=in_specs, out_specs=out_specs, check_vma=False)
```

```python
import jax
import jax.numpy as jnp
from jax import lax
from jax.sharding import Mesh, PartitionSpec as P

HEADS = 16
SPAN = 256

SEG_SPLIT = (("seg_z", 8), ("seg_y", 4), ("seg_x", 2))
SCAN_AXES = ("seg_z", "seg_y", "seg_x", "frm")


def features(t):
    return jnp.where(t > 0.0, t + 1.0, jnp.exp(jnp.minimum(t, 0.0)))


def tmap(f, *trees):
    return jax.tree.map(f, *trees)


def send(tree, axis, pairs):
    return tmap(lambda t: lax.ppermute(t, axis, perm=pairs), tree)


def swap(tree, axis):
    return send(tree, axis, [(0, 1), (1, 0)])


def forward(n, s):
    return [(i, i + s) for i in range(n - s)]


def part(tree, index, count):
    def one(t):
        size = t.shape[0] // count
        return lax.dynamic_slice_in_dim(t, index * size, size, axis=0)

    return tmap(one, tree)


def ordered(mine, other, first):
    lo = tmap(lambda a, b: jnp.where(first, a, b), mine, other)
    hi = tmap(lambda a, b: jnp.where(first, b, a), mine, other)
    return lo, hi


def keep(tree, cond):
    return tmap(lambda a: jnp.where(cond, a, jnp.zeros_like(a)), tree)


def joined(lo, hi):
    return tmap(lambda a, b: jnp.concatenate([a, b], axis=0), lo, hi)


def cyclic(n, s):
    return [(i, (i + s) % n) for i in range(n)]


def entering(total, carry):
    core = lax.axis_index("frm")
    xh = lax.axis_index("seg_x")
    y = lax.axis_index("seg_y")
    z = lax.axis_index("seg_z")
    n_y = lax.axis_size("seg_y")
    n_z = lax.axis_size("seg_z")
    add = lambda a, b: tmap(jnp.add, a, b)
    own_c = part(total, core, 2)
    got_c = swap(part(total, 1 - core, 2), "frm")
    lo, hi = ordered(own_c, got_c, core == 0)
    chip = add(lo, hi)
    came = [part(chip, y, n_y)] + [
        send(part(chip, (y + s) % n_y, n_y), "seg_y", cyclic(n_y, s)) for s in range(1, n_y)
    ]
    column = came[0]
    for c in came[1:]:
        column = add(column, c)
    assert n_z == 8
    left = send(column, "seg_z", cyclic(n_z, 1))
    right = send(column, "seg_z", cyclic(n_z, -1))
    before_z = add(keep(left, z >= 1), keep(right, z + 1 >= n_z))
    to = lambda s: (z + s) % n_z
    two = send(keep(column, to(2) >= 2), "seg_z", cyclic(n_z, 2))
    three = add(keep(column, to(3) >= 3), keep(left, to(3) >= 4))
    three = send(three, "seg_z", cyclic(n_z, 3))
    back = add(keep(column, to(-2) + 2 >= n_z), keep(right, to(-2) + 3 >= n_z))
    back = send(back, "seg_z", cyclic(n_z, -2))
    before_z = add(before_z, add(two, add(three, back)))

    def for_row(t):
        out = before_z
        for s, c in enumerate(came):
            out = add(out, keep(c, (y - s) % n_y < t))
        return out

    pieces = [for_row(y)] + [
        send(for_row((y + s) % n_y), "seg_y", cyclic(n_y, s)) for s in range(1, n_y)
    ]
    order = (y - jnp.arange(n_y)) % n_y
    mine = tmap(
        lambda *p: jnp.stack(p)[order].reshape((-1,) + p[0].shape[1:]),
        *pieces,
    )
    mine, carry = lax.optimization_barrier((mine, carry))
    half = add(mine, swap(add(mine, keep(chip, xh == 0)), "seg_x"))
    got = swap(add(half, keep(own_c, core == 0)), "frm")
    own = tmap(lambda a, c: jnp.where(core == 0, a, a + c), half, got_c)
    return (own, got), carry


def block_terms(phi_q, phi_k, values, span):
    rows, length, heads, dim = phi_q.shape
    count = length // span
    pq = phi_q.reshape(rows, count, span, heads, dim)
    pk = phi_k.reshape(rows, count, span, heads, dim)
    vv = values.reshape(rows, count, span, heads, dim)
    scores = jnp.einsum("rnihd,rnjhd->rnhij", pq, pk, preferred_element_type=jnp.float32)
    causal = jnp.arange(span)[:, None] >= jnp.arange(span)[None, :]
    scores = jnp.where(causal, scores, 0.0)
    den_local = jnp.sum(scores, axis=-1)
    weights = scores.astype(jnp.bfloat16)
    num_local = jnp.einsum("rnhij,rnjhd->rnihd", weights, vv, preferred_element_type=jnp.float32)
    kv_blocks = jnp.einsum("rnjhd,rnjhe->rnhde", pk, vv, preferred_element_type=jnp.float32)
    k_blocks = jnp.sum(pk, axis=2, dtype=jnp.float32)
    return (pq, num_local, den_local, kv_blocks, k_blocks)


def finish(pq, num_local, den_local, kv_blocks, k_blocks, prior_kv, prior_k):
    rows, count, span, heads, dim = pq.shape
    before_kv = jnp.cumsum(kv_blocks, axis=1) - kv_blocks + prior_kv[:, None]
    before_k = jnp.cumsum(k_blocks, axis=1) - k_blocks + prior_k[:, None]
    pq32 = pq.astype(jnp.float32)
    num = num_local + jnp.einsum(
        "rnihd,rnhde->rnihe", pq32, before_kv, precision=lax.Precision.HIGHEST
    )
    den = jnp.transpose(den_local, (0, 1, 3, 2)) + jnp.sum(pq32 * before_k[:, :, None], axis=-1)
    result = (num / den[..., None]).astype(jnp.bfloat16)
    return result.reshape(rows, count * span, heads * dim)


def split_qkv(qkv):
    phi_q = features(qkv[:, :, 0].astype(jnp.float32)).astype(jnp.bfloat16)
    phi_k = features(qkv[:, :, 1].astype(jnp.float32)).astype(jnp.bfloat16)
    return (phi_q, phi_k, qkv[:, :, 2])


def shards(frames_in, w_qkv, w_out):
    rows, tok_local, width = frames_in.shape
    head_dim = width // HEADS
    def project(w, count):
        out = jnp.einsum("rtd,de->ret", frames_in, w, preferred_element_type=jnp.float32)
        out = out.astype(jnp.bfloat16).reshape(rows, count, HEADS, head_dim, tok_local)
        return jnp.transpose(out, (0, 4, 1, 2, 3))

    keys_values = project(w_qkv[:, width:], 2)
    queries = project(w_qkv[:, :width], 1)
    phi_q = features(queries[:, :, 0].astype(jnp.float32)).astype(jnp.bfloat16)
    phi_k = features(keys_values[:, :, 0].astype(jnp.float32)).astype(jnp.bfloat16)
    values = keys_values[:, :, 1]
    pq, num_local, den_local, kv_blocks, k_blocks = block_terms(phi_q, phi_k, values, SPAN)
    total_kv = jnp.sum(kv_blocks, axis=1)[0]
    total_k = jnp.sum(k_blocks, axis=1)[0]
    lanes = 128
    dense = total_kv.reshape(HEADS, -1, lanes)
    rows_kv = dense.shape[1]
    norm = jnp.pad(total_k, ((0, 0), (0, lanes - total_k.shape[1])))[:, None]
    (own, other), (num_local, den_local) = entering(
        jnp.concatenate([dense, norm], axis=1), (num_local, den_local)
    )
    core = lax.axis_index("frm")
    half_heads = HEADS // 2

    def heads_of(prior, which):
        first = which * half_heads
        pick = lambda t, axis: lax.dynamic_slice_in_dim(t, first, half_heads, axis=axis)
        prior_kv = prior[:, :rows_kv].reshape((half_heads,) + total_kv.shape[1:])
        prior_k = prior[:, rows_kv, : total_k.shape[1]]
        heads_out = finish(
            pick(pq, 3), pick(num_local, 3), pick(den_local, 2),
            pick(kv_blocks, 2), pick(k_blocks, 2), prior_kv[None], prior_k[None],
        )
        rows_w = lax.dynamic_slice_in_dim(w_out, first * head_dim, half_heads * head_dim, axis=0)
        return jnp.einsum("rtd,de->rte", heads_out, rows_w, preferred_element_type=jnp.float32)

    out = heads_of(own, core) + heads_of(other, 1 - core)
    return out.astype(jnp.bfloat16)


def solution(mesh):
    sizes = [n for _, n in SEG_SPLIT]
    devices = mesh.devices.reshape(
        *sizes, mesh.shape["frm"], mesh.shape["rec"]
    )
    fine = Mesh(devices, tuple(name for name, _ in SEG_SPLIT) + ("frm", "rec"))
    in_specs = (P("rec", SCAN_AXES, None), P(), P())
    out_specs = P("rec", SCAN_AXES, None)
    return jax.shard_map(shards, mesh=fine, in_specs=in_specs, out_specs=out_specs, check_vma=False)
```
